256 devices in a mesh: comp: 2 (over core), seq: 16 (over y_lo, z), tp: 8 (over y_hi, x).
Axes of the slice: x: 4, y: 4 (y_hi: 2, y_lo: 2; y = y_hi * 2 + y_lo), z: 8, core: 2. Of those that a mesh axis runs over, the one named last changes fastest.
Arguments:
- inputs: bfloat16 [2, 8, 2048, 3072], P('comp', None, ('seq', 'tp')), may hold values from -6 to 6
- modulation: float32 [2, 8, 3, 3072], P('comp'), may hold values from -4 to 4
- w_qkv: bfloat16 [2, 3072, 3, 3072], P('comp', None, None, 'tp'), may hold values from -0.108253175 to 0.108253175
- w_attn_out: bfloat16 [2, 3072, 3072], P('comp', 'tp'), may hold values from -0.109375 to 0.109375
- qk_gain: float32 [2, 2, 128], P('comp'), may hold values from 1 to 5
- final_mod: float32 [8, 2, 3072], replicated, may hold values from -4 to 4
- w_final: bfloat16 [3072, 64], replicated, may hold values from -0.109375 to 0.109375
- w_embed: bfloat16 [64, 3072], replicated, may hold values from -0.75 to 0.75
- latent: float32 [8, 64, 2048], P(None, None, ('seq', 'tp')), may hold values from -6 to 6
Outputs:
- handed: bfloat16 [2, 8, 2048, 3072], P('comp', None, ('seq', 'tp'))
- velocity: float32 [8, 64, 2048], P(None, None, ('seq', 'tp'))
- advanced: float32 [8, 64, 2048], P(None, None, ('seq', 'tp'))
The draws below stay inside these ranges and needn't reach their ends.
All inputs are finite; a program needn't handle non-finite values.
Results may differ from the reference program's by a relative error of at most 0.011.
Values may be sent and summed in bfloat16 or wider, within the bound.
No kernel may reach another device: no remote copies, remote signals or barrier semaphores. Data moves between devices by JAX's collectives and lax.ppermute only.
A program may use at most 192 MiB of HBM per device.

```python
import math
import jax
import jax.numpy as jnp
from jax import lax

D = 3072
HEADS = 24
HD = 128
CL = 64
SAMPLES = 8
COMP = 2
TOKENS = 2048


def draw_w_qkv(key, part):
    base = jax.random.truncated_normal(key, -5.9, 5.9, (COMP, D, 3, D), jnp.float32) * D ** (-0.5)
    return base.astype(jnp.bfloat16)


def draw_qk_gain(key, part):
    low_end, high_end = (math.log(1.2), math.log(2.2))
    return jnp.exp(jax.random.uniform(key, (COMP, 2, HD), jnp.float32, low_end, high_end))


def block_scale(rng, extent, split, smallest, high):
    def one(dim, blocks):
        steps = jax.random.uniform(jax.random.fold_in(jax.random.fold_in(rng, 6), dim), (blocks,), jnp.float32, smallest / len(split), high / len(split))
        return jnp.repeat(jnp.exp(steps), extent[dim] // blocks).reshape((-1,) + (1,) * (len(extent) - dim - 1))

    level = one(*split[0])
    for cut in split[1:]:
        level = level * one(*cut)
    return level


def normal_values(stream_key, extent, scale, limit, split=(), held_as=jnp.bfloat16):
    values = scale * jax.random.normal(stream_key, extent, jnp.float32)
    if split:
        values = values * block_scale(stream_key, extent, split, -0.22, 0.18)
    return jnp.clip(values, -limit, limit).astype(held_as)


def setup_inputs(seed: int = 0) -> dict:
    splits = jax.random.split(jax.random.key(seed), 10)
    inputs = normal_values(splits[0], (COMP, SAMPLES, TOKENS, D), 1.0, 6.0, ((0, 2), (2, 128)))
    modulation = normal_values(splits[1], (COMP, SAMPLES, 3, D), 0.8, 4.0, ((0, 2),), jnp.float32)
    w_qkv = draw_w_qkv(jax.random.fold_in(splits[9], 71), 0)
    w_attn_out = normal_values(splits[3], (COMP, D, D), D ** -0.5, 0.109375, ((0, 2), (1, 8)))
    qk_gain = draw_qk_gain(jax.random.fold_in(splits[9], 71), 0)
    final_mod = normal_values(splits[5], (SAMPLES, 2, D), 0.8, 4.0, (), jnp.float32)
    w_final = normal_values(splits[6], (D, CL), D ** -0.5, 0.109375)
    w_embed = normal_values(splits[7], (CL, D), CL ** -0.5, 0.75)
    latent = normal_values(splits[8], (SAMPLES, CL, TOKENS), 1.0, 6.0, ((2, 128),), jnp.float32)
    return {"inputs": inputs, "modulation": modulation, "w_qkv": w_qkv, "w_attn_out": w_attn_out, "qk_gain": qk_gain, "final_mod": final_mod, "w_final": w_final, "w_embed": w_embed, "latent": latent}


step_size = 0.02
norm_eps = 1e-06

def layer_norm(values):
    center = values - lax.optimization_barrier(jnp.mean(values, -1, keepdims=True))
    return center * lax.rsqrt(lax.optimization_barrier(jnp.mean(center * center, -1, keepdims=True)) + norm_eps)

def rms_norm(values, norm_gain):
    return values * lax.rsqrt(lax.optimization_barrier(jnp.mean(values * values, -1, keepdims=True)) + norm_eps) * norm_gain

def attend(queried, keyed_rows, valued):
    scaling = HD ** (-0.5)
    block_rows = math.gcd(TOKENS, 512)
    keys_float = keyed_rows.astype(jnp.float32)
    values_float = valued.astype(jnp.float32)

    def one_block(query_block):
        scores = jnp.einsum('qhd,khd->qhk', query_block.astype(jnp.float32), keys_float) * scaling
        row_max = lax.optimization_barrier(jnp.max(scores, -1, keepdims=True))
        weight = jnp.exp(scores - row_max)
        weight_sum = lax.optimization_barrier(jnp.sum(weight, -1))
        rounded = lax.optimization_barrier(weight.astype(jnp.bfloat16)).astype(jnp.float32)
        summed = jnp.einsum('qhk,khd->qhd', rounded, values_float)
        return (summed / weight_sum[..., None]).astype(jnp.bfloat16)
    blocks = lax.map(one_block, queried.reshape(TOKENS // block_rows, block_rows, HEADS, HD))
    return blocks.reshape(TOKENS, HEADS, HD)

def component(x_rows, mod_rows, weights, out_weights, norm_gains):
    x_float = x_rows.astype(jnp.float32)
    x_mod = (layer_norm(x_float) * (1.0 + mod_rows[:, 1, None, :]) + mod_rows[:, 0, None, :]).astype(jnp.bfloat16)
    mixed_rows = jnp.dot(x_mod.reshape(SAMPLES * TOKENS, D), weights.reshape(D, 3 * D), preferred_element_type=jnp.float32)
    mixed_rows = mixed_rows.reshape(SAMPLES, TOKENS, 3, HEADS, HD)
    queried = rms_norm(mixed_rows[:, :, 0], norm_gains[0]).astype(jnp.bfloat16)
    keyed_rows = rms_norm(mixed_rows[:, :, 1], norm_gains[1]).astype(jnp.bfloat16)
    valued = mixed_rows[:, :, 2].astype(jnp.bfloat16)
    attended = lax.map(lambda packed: attend(*packed), (queried, keyed_rows, valued))
    branch = jnp.dot(attended.reshape(SAMPLES * TOKENS, D), out_weights, preferred_element_type=jnp.float32)
    branch = branch.reshape(SAMPLES, TOKENS, D)
    return (x_float + mod_rows[:, 2, None, :] * branch).astype(jnp.bfloat16)

def reference(inputs, modulation, w_qkv, w_attn_out, qk_gain, final_mod, w_final, w_embed, latent):
    outputs = lax.map(lambda packed: component(*packed), (inputs, modulation, w_qkv, w_attn_out, qk_gain))
    last_out = outputs[COMP - 1].astype(jnp.float32)
    final_in = (layer_norm(last_out) * (1.0 + final_mod[:, 1, None, :]) + final_mod[:, 0, None, :]).astype(jnp.bfloat16)
    projected = jnp.dot(final_in.reshape(SAMPLES * TOKENS, D), w_final, preferred_element_type=jnp.float32)
    velocity = projected.reshape(SAMPLES, TOKENS, CL).transpose(0, 2, 1)
    advanced = latent + step_size * velocity
    flat_latent = advanced.transpose(0, 2, 1).reshape(SAMPLES * TOKENS, CL).astype(jnp.bfloat16)
    embedded = jnp.dot(flat_latent, w_embed, preferred_element_type=jnp.float32).astype(jnp.bfloat16)
    embedded = embedded.reshape(SAMPLES, TOKENS, D)
    handed = jnp.concatenate([embedded[None], outputs[:-1]], 0)
    return (handed, velocity, advanced)
```

```python
import jax
import jax.numpy as jnp
from jax import lax
from jax.sharding import PartitionSpec as P

step_size = 0.02
norm_eps = 1e-06


def broadcast(block, axis, owner):
    block = jnp.where(lax.axis_index(axis) == owner, block, jnp.zeros_like(block))
    return lax.psum(block, axis)


def shifted(block, axis, distance):
    devices = range(lax.axis_size(axis))
    route = [((i - distance) % len(devices), i) for i in devices]
    return lax.ppermute(block, axis, route)


def layer_norm(values):
    center = values - jnp.mean(values, -1, keepdims=True)
    return center * lax.rsqrt(jnp.mean(center * center, -1, keepdims=True) + norm_eps)


def rms_norm(values, norm_gain):
    return values * lax.rsqrt(jnp.mean(values * values, -1, keepdims=True) + norm_eps) * norm_gain


def body(inputs, modulation, w_qkv, w_attn_out, qk_gain, final_mod, w_final, w_embed, latent):
    head_dim = qk_gain.shape[2]
    x_rows = inputs[0]
    samples, tokens_local, width = x_rows.shape
    n_seq = lax.axis_size("seq")
    parts = n_seq // samples
    part_tokens = tokens_local // parts
    mod_rows = modulation[0]
    x_float = x_rows.astype(jnp.float32)
    x_mod = (
        layer_norm(x_float) * (1.0 + mod_rows[:, 1, None, :]) + mod_rows[:, 0, None, :]
    ).astype(jnp.bfloat16)
    x_parts = x_mod.reshape(samples * parts, part_tokens, width)
    x_clip = lax.all_to_all(x_parts, "seq", 0, 0, tiled=True)
    x_group = lax.all_gather(x_clip, "tp", axis=0, tiled=False)
    n_tp, n_src = x_group.shape[0], x_group.shape[1]
    rows = n_tp * n_src * part_tokens
    weights = w_qkv[0]
    local_width = weights.shape[2]
    heads_local = local_width // head_dim
    norm_gains = qk_gain[0]
    scaling = head_dim ** (-0.5)
    mixed_rows = jnp.einsum(
        "rd,dje->rje",
        x_group.reshape(rows, width),
        weights,
        preferred_element_type=jnp.float32,
    )
    unpacked = mixed_rows.reshape(rows, 3, heads_local, head_dim)
    queried = rms_norm(unpacked[:, 0], norm_gains[0]).astype(jnp.bfloat16)
    keyed_rows = rms_norm(unpacked[:, 1], norm_gains[1]).astype(jnp.bfloat16)
    pairs = jnp.stack([keyed_rows, unpacked[:, 2].astype(jnp.bfloat16)], 0)
    partner = [(i, i ^ 1) for i in range(n_seq)]
    other = lax.ppermute(pairs, "seq", partner)
    all_pairs = jnp.concatenate([pairs, other], 1)
    scores = (
        jnp.einsum(
            "qhd,khd->hqk", queried, all_pairs[0], preferred_element_type=jnp.float32
        )
        * scaling
    )
    row_max = jnp.max(scores, -1)
    weight = jnp.exp(scores - row_max[..., None])
    row_sum = jnp.sum(weight, -1)
    summed = jnp.einsum(
        "hqk,khd->qhd",
        weight.astype(jnp.bfloat16),
        all_pairs[1],
        preferred_element_type=jnp.float32,
    )
    attended = (
        (summed / jnp.transpose(row_sum)[..., None])
        .astype(jnp.bfloat16)
        .reshape(rows, local_width)
    )
    partial_out = jnp.einsum(
        "re,ed->rd", attended, w_attn_out[0], preferred_element_type=jnp.float32
    )
    branch_clip = lax.psum_scatter(
        partial_out.astype(jnp.bfloat16).reshape(n_tp, n_src * part_tokens, width),
        "tp",
        scatter_dimension=0,
        tiled=True,
    ).reshape(n_src, part_tokens, width)
    branch = (
        lax.all_to_all(branch_clip, "seq", 0, 0, tiled=True)
        .reshape(samples, tokens_local, width)
        .astype(jnp.float32)
    )
    output = (x_float + mod_rows[:, 2, None, :] * branch).astype(jnp.bfloat16)
    final_in = (
        layer_norm(output.astype(jnp.float32)) * (1.0 + final_mod[:, 1, None, :])
        + final_mod[:, 0, None, :]
    ).astype(jnp.bfloat16)
    velocity = jnp.einsum("srd,dc->scr", final_in, w_final, preferred_element_type=jnp.float32)
    advanced = latent + step_size * velocity
    last_comp = lax.axis_size("comp") - 1
    position = lax.axis_index("comp")
    shared = broadcast(
        jnp.stack([velocity, advanced]).astype(jnp.bfloat16), "comp", last_comp
    ).astype(jnp.float32)
    embedded = jnp.einsum(
        "scr,cd->srd", advanced.astype(jnp.bfloat16), w_embed, preferred_element_type=jnp.float32
    ).astype(jnp.bfloat16)
    sending = jnp.where(position == last_comp, embedded, output)
    handed = shifted(sending, "comp", 1)
    return (handed[None], shared[0], shared[1])


def solution(mesh):
    in_specs = (
        P("comp", None, ("seq", "tp"), None),
        P("comp", None, None, None),
        P("comp", None, None, "tp"),
        P("comp", "tp", None),
        P("comp", None, None),
        P(),
        P(),
        P(),
        P(None, None, ("seq", "tp")),
    )
    out_specs = (
        P("comp", None, ("seq", "tp"), None),
        P(None, None, ("seq", "tp")),
        P(None, None, ("seq", "tp")),
    )
    return jax.shard_map(body, mesh=mesh, in_specs=in_specs, out_specs=out_specs, check_vma=False)
```

```python
import jax
import jax.numpy as jnp
from jax import lax
import functools
from jax.experimental import pallas as pl
from jax.experimental.pallas import tpu as pltpu
from jax.sharding import PartitionSpec as P

step_size = 0.02
norm_eps = 1e-06


def broadcast(block, axis, owner):
    block = jnp.where(lax.axis_index(axis) == owner, block, jnp.zeros_like(block))
    return lax.psum(block, axis)


def shifted(block, axis, distance):
    devices = range(lax.axis_size(axis))
    route = [((i - distance) % len(devices), i) for i in devices]
    return lax.ppermute(block, axis, route)


def layer_norm(values):
    center = values - jnp.mean(values, -1, keepdims=True)
    return center * lax.rsqrt(jnp.mean(center * center, -1, keepdims=True) + norm_eps)


def rms_norm(values, norm_gain):
    return values * lax.rsqrt(jnp.mean(values * values, -1, keepdims=True) + norm_eps) * norm_gain


def _project_kernel(x_ref, w_ref, g_ref, o_ref, *, heads):
    which = pl.program_id(0) // heads
    mixed = jnp.dot(x_ref[...], w_ref[...], preferred_element_type=jnp.float32)
    normed = (
        mixed
        * lax.rsqrt(jnp.mean(mixed * mixed, -1, keepdims=True) + norm_eps)
        * g_ref[pl.ds(which, 1), :]
    )
    o_ref[...] = jnp.where(which < 2, normed, mixed).astype(o_ref.dtype)


def project(x, w, gains, head_dim):
    rows, width = x.shape
    local_width = w.shape[2]
    heads = local_width // head_dim
    kernel = functools.partial(_project_kernel, heads=heads)
    return pl.pallas_call(
        kernel,
        grid=(3 * heads,),
        in_specs=[
            pl.BlockSpec((rows, width), lambda c: (0, 0)),
            pl.BlockSpec((None, width, head_dim), lambda c: (c // heads, 0, c % heads)),
            pl.BlockSpec(gains.shape, lambda c: (0, 0)),
        ],
        out_specs=pl.BlockSpec(
            (None, rows, head_dim), lambda c: (c // heads, 0, c % heads)
        ),
        out_shape=jax.ShapeDtypeStruct((3, rows, local_width), jnp.bfloat16),
        compiler_params=pltpu.CompilerParams(vmem_limit_bytes=48 * 1024 * 1024),
    )(x, w, gains)


def _attend_kernel(q_ref, k_ref, v_ref, ko_ref, vo_ref, o_ref, *, scaling):
    def scores_of(keys):
        return lax.dot_general(
            q_ref[...], keys[...], (((1,), (1,)), ((), ())), preferred_element_type=jnp.float32
        ) * scaling

    own = scores_of(k_ref)
    far = scores_of(ko_ref)
    row_max = jnp.maximum(jnp.max(own, -1, keepdims=True), jnp.max(far, -1, keepdims=True))
    own = jnp.exp(own - row_max)
    far = jnp.exp(far - row_max)
    row_sum = jnp.sum(own, -1, keepdims=True) + jnp.sum(far, -1, keepdims=True)
    summed = jnp.dot(
        own.astype(jnp.bfloat16), v_ref[...], preferred_element_type=jnp.float32
    ) + jnp.dot(far.astype(jnp.bfloat16), vo_ref[...], preferred_element_type=jnp.float32)
    o_ref[...] = (summed / row_sum).astype(o_ref.dtype)


def attend(qkv, other, head_dim, block_q=512):
    rows, width = qkv.shape[1], qkv.shape[2]
    keys = other.shape[1]
    heads = width // head_dim
    kernel = functools.partial(_attend_kernel, scaling=head_dim ** (-0.5))

    def part(index, extent):
        return pl.BlockSpec((None, extent, head_dim), lambda h, i: (index, 0, h))

    return pl.pallas_call(
        kernel,
        grid=(heads, rows // block_q),
        in_specs=[
            pl.BlockSpec((None, block_q, head_dim), lambda h, i: (0, i, h)),
            part(1, rows),
            part(2, rows),
            part(0, keys),
            part(1, keys),
        ],
        out_specs=pl.BlockSpec((block_q, head_dim), lambda h, i: (i, h)),
        out_shape=jax.ShapeDtypeStruct((rows, width), jnp.bfloat16),
        compiler_params=pltpu.CompilerParams(vmem_limit_bytes=48 * 1024 * 1024),
    )(qkv, qkv, qkv, other, other)


def body(inputs, modulation, w_qkv, w_attn_out, qk_gain, final_mod, w_final, w_embed, latent):
    head_dim = qk_gain.shape[2]
    x_rows = inputs[0]
    samples, tokens_local, width = x_rows.shape
    n_seq = lax.axis_size("seq")
    parts = n_seq // samples
    part_tokens = tokens_local // parts
    mod_rows = modulation[0]
    x_float = x_rows.astype(jnp.float32)
    x_mod = (
        layer_norm(x_float) * (1.0 + mod_rows[:, 1, None, :]) + mod_rows[:, 0, None, :]
    ).astype(jnp.bfloat16)
    x_parts = x_mod.reshape(samples * parts, part_tokens, width)
    x_clip = lax.all_to_all(x_parts, "seq", 0, 0, tiled=True)
    x_group = lax.all_gather(x_clip, "tp", axis=0, tiled=False)
    n_tp, n_src = x_group.shape[0], x_group.shape[1]
    rows = n_tp * n_src * part_tokens
    weights = w_qkv[0]
    local_width = weights.shape[2]
    heads_local = local_width // head_dim
    norm_gains = qk_gain[0]
    gains = jnp.concatenate([norm_gains, jnp.ones_like(norm_gains[:1])], 0)
    qkv = project(
        x_group.reshape(rows, width), jnp.transpose(weights, (1, 0, 2)), gains, head_dim
    )
    partner = [(i, i ^ 1) for i in range(n_seq)]
    other = lax.ppermute(qkv[1:], "seq", partner)
    attended = attend(qkv, other, head_dim)
    partial_out = jnp.einsum(
        "re,ed->rd", attended, w_attn_out[0], preferred_element_type=jnp.float32
    )
    branch_clip = lax.psum_scatter(
        partial_out.astype(jnp.bfloat16).reshape(n_tp, n_src * part_tokens, width),
        "tp",
        scatter_dimension=0,
        tiled=True,
    ).reshape(n_src, part_tokens, width)
    branch = (
        lax.all_to_all(branch_clip, "seq", 0, 0, tiled=True)
        .reshape(samples, tokens_local, width)
        .astype(jnp.float32)
    )
    output = (x_float + mod_rows[:, 2, None, :] * branch).astype(jnp.bfloat16)
    final_in = (
        layer_norm(output.astype(jnp.float32)) * (1.0 + final_mod[:, 1, None, :])
        + final_mod[:, 0, None, :]
    ).astype(jnp.bfloat16)
    velocity = jnp.einsum("srd,dc->scr", final_in, w_final, preferred_element_type=jnp.float32)
    advanced = latent + step_size * velocity
    last_comp = lax.axis_size("comp") - 1
    position = lax.axis_index("comp")
    shared = broadcast(
        jnp.stack([velocity, advanced]).astype(jnp.bfloat16), "comp", last_comp
    ).astype(jnp.float32)
    embedded = jnp.einsum(
        "scr,cd->srd", advanced.astype(jnp.bfloat16), w_embed, preferred_element_type=jnp.float32
    ).astype(jnp.bfloat16)
    sending = jnp.where(position == last_comp, embedded, output)
    handed = shifted(sending, "comp", 1)
    return (handed[None], shared[0], shared[1])


def solution(mesh):
    in_specs = (
        P("comp", None, ("seq", "tp"), None),
        P("comp", None, None, None),
        P("comp", None, None, "tp"),
        P("comp", "tp", None),
        P("comp", None, None),
        P(),
        P(),
        P(),
        P(None, None, ("seq", "tp")),
    )
    out_specs = (
        P("comp", None, ("seq", "tp"), None),
        P(None, None, ("seq", "tp")),
        P(None, None, ("seq", "tp")),
    )
    return jax.shard_map(body, mesh=mesh, in_specs=in_specs, out_specs=out_specs, check_vma=False)
```

```python
import jax
import jax.numpy as jnp
from jax import lax
import functools
from jax.experimental import pallas as pl
from jax.experimental.pallas import tpu as pltpu
from jax.sharding import PartitionSpec as P

step_size = 0.02
norm_eps = 1e-06


def broadcast(block, axis, owner):
    block = jnp.where(lax.axis_index(axis) == owner, block, jnp.zeros_like(block))
    return lax.psum(block, axis)


def shifted(block, axis, distance):
    devices = range(lax.axis_size(axis))
    route = [((i - distance) % len(devices), i) for i in devices]
    return lax.ppermute(block, axis, route)


def layer_norm(values):
    center = values - jnp.mean(values, -1, keepdims=True)
    return center * lax.rsqrt(jnp.mean(center * center, -1, keepdims=True) + norm_eps)


def rms_norm(values, norm_gain):
    return values * lax.rsqrt(jnp.mean(values * values, -1, keepdims=True) + norm_eps) * norm_gain


def _project_kernel(x_ref, w_ref, g_ref, o_ref, *, heads, head_dim):
    which = pl.program_id(0)
    mixed = jnp.dot(x_ref[...], w_ref[...], preferred_element_type=jnp.float32)
    gain = g_ref[pl.ds(which, 1), :]
    for h in range(heads):
        block = mixed[:, h * head_dim : (h + 1) * head_dim]
        normed = (
            block * lax.rsqrt(jnp.mean(block * block, -1, keepdims=True) + norm_eps) * gain
        )
        o_ref[:, h * head_dim : (h + 1) * head_dim] = jnp.where(
            which < 2, normed, block
        ).astype(o_ref.dtype)


def project(x, w, gains, head_dim):
    rows, width = x.shape
    local_width = w.shape[2]
    heads = local_width // head_dim
    kernel = functools.partial(_project_kernel, heads=heads, head_dim=head_dim)
    return pl.pallas_call(
        kernel,
        grid=(3,),
        in_specs=[
            pl.BlockSpec((rows, width), lambda c: (0, 0)),
            pl.BlockSpec((None, width, local_width), lambda c: (c, 0, 0)),
            pl.BlockSpec(gains.shape, lambda c: (0, 0)),
        ],
        out_specs=pl.BlockSpec((None, rows, local_width), lambda c: (c, 0, 0)),
        out_shape=jax.ShapeDtypeStruct((3, rows, local_width), jnp.bfloat16),
        compiler_params=pltpu.CompilerParams(vmem_limit_bytes=48 * 1024 * 1024),
    )(x, w, gains)


def _attend_kernel(*refs, scaling, sources):
    q_ref, o_ref = refs[0], refs[-1]
    pairs = refs[1:-1]

    def scores_of(keys):
        return lax.dot_general(
            q_ref[...], keys[...], (((1,), (1,)), ((), ())), preferred_element_type=jnp.float32
        ) * scaling

    scores = [scores_of(pairs[2 * n]) for n in range(sources)]
    row_max = jnp.max(scores[0], -1, keepdims=True)
    for block in scores[1:]:
        row_max = jnp.maximum(row_max, jnp.max(block, -1, keepdims=True))
    weights = [jnp.exp(block - row_max) for block in scores]
    row_sum = sum(jnp.sum(block, -1, keepdims=True) for block in weights)
    summed = sum(
        jnp.dot(block.astype(jnp.bfloat16), pairs[2 * n + 1][...], preferred_element_type=jnp.float32)
        for n, block in enumerate(weights)
    )
    o_ref[...] = (summed / row_sum).astype(o_ref.dtype)


def attend(queries, key_sources, head_dim, block_q=512):
    rows, width = queries.shape[1], queries.shape[2]
    heads = width // head_dim
    block_q = min(block_q, rows)
    kernel = functools.partial(
        _attend_kernel, scaling=head_dim ** (-0.5), sources=len(key_sources)
    )
    in_specs = [pl.BlockSpec((None, block_q, head_dim), lambda h, i: (0, i, h))]
    operands = [queries]
    for source, first in key_sources:
        extent = source.shape[1]
        for index in (first, first + 1):
            in_specs.append(
                pl.BlockSpec((None, extent, head_dim), lambda h, i, index=index: (index, 0, h))
            )
            operands.append(source)
    return pl.pallas_call(
        kernel,
        grid=(heads, rows // block_q),
        in_specs=in_specs,
        out_specs=pl.BlockSpec((block_q, head_dim), lambda h, i: (i, h)),
        out_shape=jax.ShapeDtypeStruct((rows, width), jnp.bfloat16),
        compiler_params=pltpu.CompilerParams(vmem_limit_bytes=48 * 1024 * 1024),
    )(*operands)


def body(inputs, modulation, w_qkv, w_attn_out, qk_gain, final_mod, w_final, w_embed, latent):
    head_dim = qk_gain.shape[2]
    x_rows = inputs[0]
    samples, tokens_local, width = x_rows.shape
    n_seq = lax.axis_size("seq")
    parts = n_seq // samples
    part_tokens = tokens_local // parts
    mod_rows = modulation[0]
    x_float = x_rows.astype(jnp.float32)
    x_mod = (
        layer_norm(x_float) * (1.0 + mod_rows[:, 1, None, :]) + mod_rows[:, 0, None, :]
    ).astype(jnp.bfloat16)
    x_parts = x_mod.reshape(samples * parts, part_tokens, width)
    weights = jnp.transpose(w_qkv[0], (1, 0, 2))
    local_width = weights.shape[2]
    norm_gains = qk_gain[0]
    gains = jnp.concatenate([norm_gains, jnp.ones_like(norm_gains[:1])], 0)
    partner = [(i, i ^ 1) for i in range(n_seq)]
    chunks = 2
    chunk_tokens = part_tokens // chunks
    projected, others = [], []
    for c in range(chunks):
        x_clip = lax.all_to_all(
            x_parts[:, c * chunk_tokens : (c + 1) * chunk_tokens], "seq", 0, 0, tiled=True
        )
        x_group = lax.all_gather(x_clip, "tp", axis=0, tiled=False)
        n_tp, n_src = x_group.shape[0], x_group.shape[1]
        rows = n_tp * n_src * chunk_tokens
        qkv = project(x_group.reshape(rows, width), weights, gains, head_dim)
        projected.append(qkv)
        others.append(lax.ppermute(qkv[1:], "seq", partner))
    key_sources = [(qkv, 1) for qkv in projected] + [(other, 0) for other in others]
    pieces = []
    for c in range(chunks):
        attended = attend(projected[c], key_sources, head_dim)
        partial_out = jnp.einsum(
            "re,ed->rd", attended, w_attn_out[0], preferred_element_type=jnp.float32
        )
        branch_clip = lax.psum_scatter(
            partial_out.astype(jnp.bfloat16).reshape(n_tp, n_src * chunk_tokens, width),
            "tp",
            scatter_dimension=0,
            tiled=True,
        ).reshape(n_src, chunk_tokens, width)
        pieces.append(lax.all_to_all(branch_clip, "seq", 0, 0, tiled=True))
    branch = (
        jnp.stack(pieces, 1)
        .reshape(samples, tokens_local, width)
        .astype(jnp.float32)
    )
    output = (x_float + mod_rows[:, 2, None, :] * branch).astype(jnp.bfloat16)
    final_in = (
        layer_norm(output.astype(jnp.float32)) * (1.0 + final_mod[:, 1, None, :])
        + final_mod[:, 0, None, :]
    ).astype(jnp.bfloat16)
    velocity = jnp.einsum("srd,dc->scr", final_in, w_final, preferred_element_type=jnp.float32)
    advanced = latent + step_size * velocity
    last_comp = lax.axis_size("comp") - 1
    position = lax.axis_index("comp")
    shared = broadcast(
        jnp.stack([velocity, advanced]).astype(jnp.bfloat16), "comp", last_comp
    ).astype(jnp.float32)
    embedded = jnp.einsum(
        "scr,cd->srd", advanced.astype(jnp.bfloat16), w_embed, preferred_element_type=jnp.float32
    ).astype(jnp.bfloat16)
    sending = jnp.where(position == last_comp, embedded, output)
    handed = shifted(sending, "comp", 1)
    return (handed[None], shared[0], shared[1])


def solution(mesh):
    in_specs = (
        P("comp", None, ("seq", "tp"), None),
        P("comp", None, None, None),
        P("comp", None, None, "tp"),
        P("comp", "tp", None),
        P("comp", None, None),
        P(),
        P(),
        P(),
        P(None, None, ("seq", "tp")),
    )
    out_specs = (
        P("comp", None, ("seq", "tp"), None),
        P(None, None, ("seq", "tp")),
        P(None, None, ("seq", "tp")),
    )
    return jax.shard_map(body, mesh=mesh, in_specs=in_specs, out_specs=out_specs, check_vma=False)
```

```python
import jax
import jax.numpy as jnp
from jax import lax
import functools
from jax.experimental import pallas as pl
from jax.experimental.pallas import tpu as pltpu
from jax.sharding import PartitionSpec as P

step_size = 0.02
norm_eps = 1e-06


def broadcast(block, axis, owner):
    block = jnp.where(lax.axis_index(axis) == owner, block, jnp.zeros_like(block))
    return lax.psum(block, axis)


def shifted(block, axis, distance):
    devices = range(lax.axis_size(axis))
    route = [((i - distance) % len(devices), i) for i in devices]
    return lax.ppermute(block, axis, route)


def layer_norm(values):
    center = values - jnp.mean(values, -1, keepdims=True)
    return center * lax.rsqrt(jnp.mean(center * center, -1, keepdims=True) + norm_eps)


def rms_norm(values, norm_gain):
    return values * lax.rsqrt(jnp.mean(values * values, -1, keepdims=True) + norm_eps) * norm_gain


def _project_kernel(x_ref, w_ref, g_ref, o_ref, *, heads, head_dim, first):
    which = pl.program_id(0) + first
    mixed = jnp.dot(x_ref[...], w_ref[...], preferred_element_type=jnp.float32)
    gain = g_ref[pl.ds(which, 1), :]
    for h in range(heads):
        block = mixed[:, h * head_dim : (h + 1) * head_dim]
        normed = (
            block * lax.rsqrt(jnp.mean(block * block, -1, keepdims=True) + norm_eps) * gain
        )
        o_ref[:, h * head_dim : (h + 1) * head_dim] = jnp.where(
            which < 2, normed, block
        ).astype(o_ref.dtype)


def project(x, w, gains, head_dim, first, count):
    rows, width = x.shape
    local_width = w.shape[2]
    heads = local_width // head_dim
    kernel = functools.partial(_project_kernel, heads=heads, head_dim=head_dim, first=first)
    return pl.pallas_call(
        kernel,
        grid=(count,),
        in_specs=[
            pl.BlockSpec((rows, width), lambda c: (0, 0)),
            pl.BlockSpec((None, width, local_width), lambda c: (c + first, 0, 0)),
            pl.BlockSpec(gains.shape, lambda c: (0, 0)),
        ],
        out_specs=pl.BlockSpec((None, rows, local_width), lambda c: (c, 0, 0)),
        out_shape=jax.ShapeDtypeStruct((count, rows, local_width), jnp.bfloat16),
        compiler_params=pltpu.CompilerParams(vmem_limit_bytes=48 * 1024 * 1024),
    )(x, w, gains)


def _attend_kernel(*refs, scaling, sources):
    q_ref, o_ref = refs[0], refs[-1]
    pairs = refs[1:-1]

    def scores_of(keys):
        return lax.dot_general(
            q_ref[...], keys[...], (((1,), (1,)), ((), ())), preferred_element_type=jnp.float32
        ) * scaling

    scores = [scores_of(pairs[2 * n]) for n in range(sources)]
    row_max = jnp.max(scores[0], -1, keepdims=True)
    for block in scores[1:]:
        row_max = jnp.maximum(row_max, jnp.max(block, -1, keepdims=True))
    weights = [jnp.exp(block - row_max) for block in scores]
    row_sum = sum(jnp.sum(block, -1, keepdims=True) for block in weights)
    summed = sum(
        jnp.dot(block.astype(jnp.bfloat16), pairs[2 * n + 1][...], preferred_element_type=jnp.float32)
        for n, block in enumerate(weights)
    )
    o_ref[...] = (summed / row_sum).astype(o_ref.dtype)


def attend(queries, key_sources, head_dim, block_q=512):
    rows, width = queries.shape[1], queries.shape[2]
    heads = width // head_dim
    block_q = min(block_q, rows)
    kernel = functools.partial(
        _attend_kernel, scaling=head_dim ** (-0.5), sources=len(key_sources)
    )
    in_specs = [pl.BlockSpec((None, block_q, head_dim), lambda h, i: (0, i, h))]
    operands = [queries]
    for source, first in key_sources:
        extent = source.shape[1]
        for index in (first, first + 1):
            in_specs.append(
                pl.BlockSpec((None, extent, head_dim), lambda h, i, index=index: (index, 0, h))
            )
            operands.append(source)
    return pl.pallas_call(
        kernel,
        grid=(heads, rows // block_q),
        in_specs=in_specs,
        out_specs=pl.BlockSpec((block_q, head_dim), lambda h, i: (i, h)),
        out_shape=jax.ShapeDtypeStruct((rows, width), jnp.bfloat16),
        compiler_params=pltpu.CompilerParams(vmem_limit_bytes=48 * 1024 * 1024),
    )(*operands)


def body(inputs, modulation, w_qkv, w_attn_out, qk_gain, final_mod, w_final, w_embed, latent):
    head_dim = qk_gain.shape[2]
    x_rows = inputs[0]
    samples, tokens_local, width = x_rows.shape
    n_seq = lax.axis_size("seq")
    parts = n_seq // samples
    part_tokens = tokens_local // parts
    mod_rows = modulation[0]
    x_float = x_rows.astype(jnp.float32)
    x_mod = (
        layer_norm(x_float) * (1.0 + mod_rows[:, 1, None, :]) + mod_rows[:, 0, None, :]
    ).astype(jnp.bfloat16)
    x_parts = x_mod.reshape(samples * parts, part_tokens, width)
    weights = jnp.transpose(w_qkv[0], (1, 0, 2))
    local_width = weights.shape[2]
    norm_gains = qk_gain[0]
    gains = jnp.concatenate([norm_gains, jnp.ones_like(norm_gains[:1])], 0)
    partner = [(i, i ^ 1) for i in range(n_seq)]
    x_clip = lax.all_to_all(x_parts, "seq", 0, 0, tiled=True)
    x_group = lax.all_gather(x_clip, "tp", axis=0, tiled=False)
    n_tp, n_src = x_group.shape[0], x_group.shape[1]
    rows = n_tp * n_src * part_tokens
    x_group = x_group.reshape(rows, width)
    pairs = project(x_group, weights, gains, head_dim, 1, 2)
    other = lax.ppermute(pairs, "seq", partner)
    queried = project(x_group, weights, gains, head_dim, 0, 1)
    attended = attend(queried, [(pairs, 0), (other, 0)], head_dim)
    partial_out = jnp.einsum(
        "re,ed->rd", attended, w_attn_out[0], preferred_element_type=jnp.float32
    )
    branch_clip = lax.psum_scatter(
        partial_out.astype(jnp.bfloat16).reshape(n_tp, n_src * part_tokens, width),
        "tp",
        scatter_dimension=0,
        tiled=True,
    ).reshape(n_src, part_tokens, width)
    branch = (
        lax.all_to_all(branch_clip, "seq", 0, 0, tiled=True)
        .reshape(samples, tokens_local, width)
        .astype(jnp.float32)
    )
    output = (x_float + mod_rows[:, 2, None, :] * branch).astype(jnp.bfloat16)
    final_in = (
        layer_norm(output.astype(jnp.float32)) * (1.0 + final_mod[:, 1, None, :])
        + final_mod[:, 0, None, :]
    ).astype(jnp.bfloat16)
    velocity = jnp.einsum("srd,dc->scr", final_in, w_final, preferred_element_type=jnp.float32)
    advanced = latent + step_size * velocity
    last_comp = lax.axis_size("comp") - 1
    position = lax.axis_index("comp")
    shared = broadcast(
        jnp.stack([velocity, advanced]).astype(jnp.bfloat16), "comp", last_comp
    ).astype(jnp.float32)
    embedded = jnp.einsum(
        "scr,cd->srd", advanced.astype(jnp.bfloat16), w_embed, preferred_element_type=jnp.float32
    ).astype(jnp.bfloat16)
    sending = jnp.where(position == last_comp, embedded, output)
    handed = shifted(sending, "comp", 1)
    return (handed[None], shared[0], shared[1])


def solution(mesh):
    in_specs = (
        P("comp", None, ("seq", "tp"), None),
        P("comp", None, None, None),
        P("comp", None, None, "tp"),
        P("comp", "tp", None),
        P("comp", None, None),
        P(),
        P(),
        P(),
        P(None, None, ("seq", "tp")),
    )
    out_specs = (
        P("comp", None, ("seq", "tp"), None),
        P(None, None, ("seq", "tp")),
        P(None, None, ("seq", "tp")),
    )
    return jax.shard_map(body, mesh=mesh, in_specs=in_specs, out_specs=out_specs, check_vma=False)
```

```python
import jax
import jax.numpy as jnp
from jax import lax
import functools
from jax.experimental import pallas as pl
from jax.experimental.pallas import tpu as pltpu
from jax.sharding import PartitionSpec as P

step_size = 0.02
norm_eps = 1e-06


def broadcast(block, axis, owner):
    block = jnp.where(lax.axis_index(axis) == owner, block, jnp.zeros_like(block))
    return lax.psum(block, axis)


def shifted(block, axis, distance):
    devices = range(lax.axis_size(axis))
    route = [((i - distance) % len(devices), i) for i in devices]
    return lax.ppermute(block, axis, route)


def layer_norm(values):
    center = values - jnp.mean(values, -1, keepdims=True)
    return center * lax.rsqrt(jnp.mean(center * center, -1, keepdims=True) + norm_eps)


def rms_norm(values, norm_gain):
    return values * lax.rsqrt(jnp.mean(values * values, -1, keepdims=True) + norm_eps) * norm_gain


def _project_kernel(x_ref, w_ref, g_ref, o_ref, *, heads, head_dim, first):
    which = pl.program_id(0) + first
    mixed = jnp.dot(x_ref[...], w_ref[...], preferred_element_type=jnp.float32)
    gain = g_ref[pl.ds(which, 1), :]
    for h in range(heads):
        block = mixed[:, h * head_dim : (h + 1) * head_dim]
        normed = (
            block * lax.rsqrt(jnp.mean(block * block, -1, keepdims=True) + norm_eps) * gain
        )
        o_ref[:, h * head_dim : (h + 1) * head_dim] = jnp.where(
            which < 2, normed, block
        ).astype(o_ref.dtype)


def project(x, w, gains, head_dim, first, count):
    rows, width = x.shape
    local_width = w.shape[2]
    heads = local_width // head_dim
    kernel = functools.partial(_project_kernel, heads=heads, head_dim=head_dim, first=first)
    return pl.pallas_call(
        kernel,
        grid=(count,),
        in_specs=[
            pl.BlockSpec((rows, width), lambda c: (0, 0)),
            pl.BlockSpec((None, width, local_width), lambda c: (c + first, 0, 0)),
            pl.BlockSpec(gains.shape, lambda c: (0, 0)),
        ],
        out_specs=pl.BlockSpec((None, rows, local_width), lambda c: (c, 0, 0)),
        out_shape=jax.ShapeDtypeStruct((count, rows, local_width), jnp.bfloat16),
        compiler_params=pltpu.CompilerParams(vmem_limit_bytes=48 * 1024 * 1024),
    )(x, w, gains)


def _attend_kernel(*refs, scaling, sources):
    q_ref, o_ref = refs[0], refs[-1]
    pairs = refs[1:-1]

    def scores_of(keys):
        return lax.dot_general(
            q_ref[...], keys[...], (((1,), (1,)), ((), ())), preferred_element_type=jnp.float32
        ) * scaling

    scores = [scores_of(pairs[2 * n]) for n in range(sources)]
    row_max = jnp.max(scores[0], -1, keepdims=True)
    for block in scores[1:]:
        row_max = jnp.maximum(row_max, jnp.max(block, -1, keepdims=True))
    weights = [jnp.exp(block - row_max) for block in scores]
    row_sum = sum(jnp.sum(block, -1, keepdims=True) for block in weights)
    summed = sum(
        jnp.dot(block.astype(jnp.bfloat16), pairs[2 * n + 1][...], preferred_element_type=jnp.float32)
        for n, block in enumerate(weights)
    )
    o_ref[...] = (summed / row_sum).astype(o_ref.dtype)


def attend(queries, key_sources, head_dim, block_q=512):
    rows, width = queries.shape[1], queries.shape[2]
    heads = width // head_dim
    block_q = min(block_q, rows)
    kernel = functools.partial(
        _attend_kernel, scaling=head_dim ** (-0.5), sources=len(key_sources)
    )
    in_specs = [pl.BlockSpec((None, block_q, head_dim), lambda h, i: (0, i, h))]
    operands = [queries]
    for source, first in key_sources:
        extent = source.shape[1]
        for index in (first, first + 1):
            in_specs.append(
                pl.BlockSpec((None, extent, head_dim), lambda h, i, index=index: (index, 0, h))
            )
            operands.append(source)
    return pl.pallas_call(
        kernel,
        grid=(heads, rows // block_q),
        in_specs=in_specs,
        out_specs=pl.BlockSpec((block_q, head_dim), lambda h, i: (i, h)),
        out_shape=jax.ShapeDtypeStruct((rows, width), jnp.bfloat16),
        compiler_params=pltpu.CompilerParams(vmem_limit_bytes=48 * 1024 * 1024),
    )(*operands)


def body(inputs, modulation, w_qkv, w_attn_out, qk_gain, final_mod, w_final, w_embed, latent):
    head_dim = qk_gain.shape[2]
    x_rows = inputs[0]
    samples, tokens_local, width = x_rows.shape
    n_seq = lax.axis_size("seq")
    parts = n_seq // samples
    mod_rows = modulation[0]
    x_float = x_rows.astype(jnp.float32)
    x_mod = (
        layer_norm(x_float) * (1.0 + mod_rows[:, 1, None, :]) + mod_rows[:, 0, None, :]
    ).astype(jnp.bfloat16)
    weights = jnp.transpose(w_qkv[0], (1, 0, 2))
    local_width = weights.shape[2]
    norm_gains = qk_gain[0]
    gains = jnp.concatenate([norm_gains, jnp.ones_like(norm_gains[:1])], 0)
    ring = n_seq // parts
    groups = [list(range(p * ring, (p + 1) * ring)) for p in range(parts)]
    partner = [(i, (i + ring) % n_seq) for i in range(n_seq)]
    x_clip = lax.all_to_all(x_mod, "seq", 0, 0, tiled=True, axis_index_groups=groups)
    x_group = lax.all_gather(x_clip, "tp", axis=0, tiled=False)
    n_tp, n_src = x_group.shape[0], x_group.shape[1]
    rows = n_tp * n_src * tokens_local
    x_group = x_group.reshape(rows, width)
    pairs = project(x_group, weights, gains, head_dim, 1, 2)
    other = lax.ppermute(pairs, "seq", partner)
    queried = project(x_group, weights, gains, head_dim, 0, 1)
    attended = attend(queried, [(pairs, 0), (other, 0)], head_dim)
    partial_out = jnp.einsum(
        "re,ed->rd", attended, w_attn_out[0], preferred_element_type=jnp.float32
    )
    branch_clip = lax.psum_scatter(
        partial_out.astype(jnp.bfloat16).reshape(n_tp, n_src * tokens_local, width),
        "tp",
        scatter_dimension=0,
        tiled=True,
    ).reshape(n_src, tokens_local, width)
    branch = (
        lax.all_to_all(branch_clip, "seq", 0, 0, tiled=True, axis_index_groups=groups)
        .reshape(samples, tokens_local, width)
        .astype(jnp.float32)
    )
    output = (x_float + mod_rows[:, 2, None, :] * branch).astype(jnp.bfloat16)
    final_in = (
        layer_norm(output.astype(jnp.float32)) * (1.0 + final_mod[:, 1, None, :])
        + final_mod[:, 0, None, :]
    ).astype(jnp.bfloat16)
    velocity = jnp.einsum("srd,dc->scr", final_in, w_final, preferred_element_type=jnp.float32)
    advanced = latent + step_size * velocity
    last_comp = lax.axis_size("comp") - 1
    position = lax.axis_index("comp")
    shared = broadcast(
        jnp.stack([velocity, advanced]).astype(jnp.bfloat16), "comp", last_comp
    ).astype(jnp.float32)
    embedded = jnp.einsum(
        "scr,cd->srd", advanced.astype(jnp.bfloat16), w_embed, preferred_element_type=jnp.float32
    ).astype(jnp.bfloat16)
    sending = jnp.where(position == last_comp, embedded, output)
    handed = shifted(sending, "comp", 1)
    return (handed[None], shared[0], shared[1])


def solution(mesh):
    in_specs = (
        P("comp", None, ("seq", "tp"), None),
        P("comp", None, None, None),
        P("comp", None, None, "tp"),
        P("comp", "tp", None),
        P("comp", None, None),
        P(),
        P(),
        P(),
        P(None, None, ("seq", "tp")),
    )
    out_specs = (
        P("comp", None, ("seq", "tp"), None),
        P(None, None, ("seq", "tp")),
        P(None, None, ("seq", "tp")),
    )
    return jax.shard_map(body, mesh=mesh, in_specs=in_specs, out_specs=out_specs, check_vma=False)
```

```python
import jax
import jax.numpy as jnp
from jax import lax
import functools
from jax.experimental import pallas as pl
from jax.experimental.pallas import tpu as pltpu
from jax.sharding import PartitionSpec as P


step_size = 0.02
norm_eps = 1e-06


def broadcast(block, axis, owner):
    block = jnp.where(lax.axis_index(axis) == owner, block, jnp.zeros_like(block))
    return lax.psum(block, axis)


def shifted(block, axis, distance):
    devices = range(lax.axis_size(axis))
    route = [((i - distance) % len(devices), i) for i in devices]
    return lax.ppermute(block, axis, route)


def layer_norm(values):
    center = values - jnp.mean(values, -1, keepdims=True)
    return center * lax.rsqrt(jnp.mean(center * center, -1, keepdims=True) + norm_eps)


def rms_norm(values, norm_gain):
    return values * lax.rsqrt(jnp.mean(values * values, -1, keepdims=True) + norm_eps) * norm_gain


def _project_kernel(x_ref, w_ref, g_ref, o_ref, *, heads, head_dim, first):
    which = pl.program_id(0) + first
    mixed = jnp.dot(x_ref[...], w_ref[...], preferred_element_type=jnp.float32)
    gain = g_ref[pl.ds(which, 1), :]
    for h in range(heads):
        block = mixed[:, h * head_dim : (h + 1) * head_dim]
        normed = (
            block * lax.rsqrt(jnp.mean(block * block, -1, keepdims=True) + norm_eps) * gain
        )
        o_ref[:, h * head_dim : (h + 1) * head_dim] = jnp.where(
            which < 2, normed, block
        ).astype(o_ref.dtype)


def project(x, w, gains, head_dim, first, count):
    rows, width = x.shape
    local_width = w.shape[2]
    heads = local_width // head_dim
    kernel = functools.partial(_project_kernel, heads=heads, head_dim=head_dim, first=first)
    return pl.pallas_call(
        kernel,
        grid=(count,),
        in_specs=[
            pl.BlockSpec((rows, width), lambda c: (0, 0)),
            pl.BlockSpec((None, width, local_width), lambda c: (c + first, 0, 0)),
            pl.BlockSpec(gains.shape, lambda c: (0, 0)),
        ],
        out_specs=pl.BlockSpec((None, rows, local_width), lambda c: (c, 0, 0)),
        out_shape=jax.ShapeDtypeStruct((count, rows, local_width), jnp.bfloat16),
        compiler_params=pltpu.CompilerParams(vmem_limit_bytes=48 * 1024 * 1024),
    )(x, w, gains)


def _attend_kernel(*refs, scaling, sources):
    q_ref, o_ref = refs[0], refs[-1]
    pairs = refs[1:-1]

    def scores_of(keys):
        return lax.dot_general(
            q_ref[...], keys[...], (((1,), (1,)), ((), ())), preferred_element_type=jnp.float32
        ) * scaling

    scores = [scores_of(pairs[2 * n]) for n in range(sources)]
    row_max = jnp.max(scores[0], -1, keepdims=True)
    for block in scores[1:]:
        row_max = jnp.maximum(row_max, jnp.max(block, -1, keepdims=True))
    weights = [jnp.exp(block - row_max) for block in scores]
    row_sum = sum(jnp.sum(block, -1, keepdims=True) for block in weights)
    summed = sum(
        jnp.dot(block.astype(jnp.bfloat16), pairs[2 * n + 1][...], preferred_element_type=jnp.float32)
        for n, block in enumerate(weights)
    )
    o_ref[...] = (summed / row_sum).astype(o_ref.dtype)


def attend(queries, key_sources, head_dim, block_q=512):
    rows, width = queries.shape[1], queries.shape[2]
    heads = width // head_dim
    block_q = min(block_q, rows)
    kernel = functools.partial(
        _attend_kernel, scaling=head_dim ** (-0.5), sources=len(key_sources)
    )
    in_specs = [pl.BlockSpec((None, block_q, head_dim), lambda h, i: (0, i, h))]
    operands = [queries]
    for source, first in key_sources:
        extent = source.shape[1]
        for index in (first, first + 1):
            in_specs.append(
                pl.BlockSpec((None, extent, head_dim), lambda h, i, index=index: (index, 0, h))
            )
            operands.append(source)
    return pl.pallas_call(
        kernel,
        grid=(heads, rows // block_q),
        in_specs=in_specs,
        out_specs=pl.BlockSpec((block_q, head_dim), lambda h, i: (i, h)),
        out_shape=jax.ShapeDtypeStruct((rows, width), jnp.bfloat16),
        compiler_params=pltpu.CompilerParams(vmem_limit_bytes=48 * 1024 * 1024),
    )(*operands)


def ring_exchange(block, axis, ring):
    count = lax.axis_size(axis)
    member = lax.axis_index(axis) % ring
    order = (member + jnp.arange(ring)) % ring
    sending = jnp.take(block, order, axis=0)
    received = [sending[0]]
    for step in range(1, ring):
        route = [(i, i - i % ring + (i % ring + step) % ring) for i in range(count)]
        received.append(lax.ppermute(sending[step], axis, route))
    return jnp.take(jnp.stack(received), (member - jnp.arange(ring)) % ring, axis=0)


def body(inputs, modulation, w_qkv, w_attn_out, qk_gain, final_mod, w_final, w_embed, latent):
    head_dim = qk_gain.shape[2]
    x_rows = inputs[0]
    samples, tokens_local, width = x_rows.shape
    n_seq = lax.axis_size("seq")
    parts = n_seq // samples
    mod_rows = modulation[0]
    x_float = x_rows.astype(jnp.float32)
    x_mod = (
        layer_norm(x_float) * (1.0 + mod_rows[:, 1, None, :]) + mod_rows[:, 0, None, :]
    ).astype(jnp.bfloat16)
    weights = jnp.transpose(w_qkv[0], (1, 0, 2))
    local_width = weights.shape[2]
    norm_gains = qk_gain[0]
    gains = jnp.concatenate([norm_gains, jnp.ones_like(norm_gains[:1])], 0)
    ring = n_seq // parts
    partner = [(i, (i + ring) % n_seq) for i in range(n_seq)]
    x_clip = ring_exchange(x_mod, "seq", ring)
    x_group = lax.all_gather(x_clip, "tp", axis=0, tiled=False)
    n_tp, n_src = x_group.shape[0], x_group.shape[1]
    rows = n_tp * n_src * tokens_local
    x_group = x_group.reshape(rows, width)
    pairs = project(x_group, weights, gains, head_dim, 1, 2)
    other = lax.ppermute(pairs, "seq", partner)
    queried = project(x_group, weights, gains, head_dim, 0, 1)
    attended = attend(queried, [(pairs, 0), (other, 0)], head_dim)
    partial_out = jnp.einsum(
        "re,ed->rd", attended, w_attn_out[0], preferred_element_type=jnp.float32
    )
    branch_clip = lax.psum_scatter(
        partial_out.astype(jnp.bfloat16).reshape(n_tp, n_src * tokens_local, width),
        "tp",
        scatter_dimension=0,
        tiled=True,
    ).reshape(n_src, tokens_local, width)
    branch = (
        ring_exchange(branch_clip, "seq", ring)
        .reshape(samples, tokens_local, width)
        .astype(jnp.float32)
    )
    output = (x_float + mod_rows[:, 2, None, :] * branch).astype(jnp.bfloat16)
    final_in = (
        layer_norm(output.astype(jnp.float32)) * (1.0 + final_mod[:, 1, None, :])
        + final_mod[:, 0, None, :]
    ).astype(jnp.bfloat16)
    velocity = jnp.einsum("srd,dc->scr", final_in, w_final, preferred_element_type=jnp.float32)
    advanced = latent + step_size * velocity
    last_comp = lax.axis_size("comp") - 1
    position = lax.axis_index("comp")
    shared = broadcast(
        jnp.stack([velocity, advanced]).astype(jnp.bfloat16), "comp", last_comp
    ).astype(jnp.float32)
    embedded = jnp.einsum(
        "scr,cd->srd", advanced.astype(jnp.bfloat16), w_embed, preferred_element_type=jnp.float32
    ).astype(jnp.bfloat16)
    sending = jnp.where(position == last_comp, embedded, output)
    handed = shifted(sending, "comp", 1)
    return (handed[None], shared[0], shared[1])


def solution(mesh):
    in_specs = (
        P("comp", None, ("seq", "tp"), None),
        P("comp", None, None, None),
        P("comp", None, None, "tp"),
        P("comp", "tp", None),
        P("comp", None, None),
        P(),
        P(),
        P(),
        P(None, None, ("seq", "tp")),
    )
    out_specs = (
        P("comp", None, ("seq", "tp"), None),
        P(None, None, ("seq", "tp")),
        P(None, None, ("seq", "tp")),
    )
    return jax.shard_map(body, mesh=mesh, in_specs=in_specs, out_specs=out_specs, check_vma=False)
```

```python
import jax
import jax.numpy as jnp
from jax import lax
import functools
from jax.experimental import pallas as pl
from jax.experimental.pallas import tpu as pltpu
from jax.sharding import PartitionSpec as P

step_size = 0.02
norm_eps = 1e-06


def broadcast(block, axis, owner):
    block = jnp.where(lax.axis_index(axis) == owner, block, jnp.zeros_like(block))
    return lax.psum(block, axis)


def shifted(block, axis, distance):
    devices = range(lax.axis_size(axis))
    route = [((i - distance) % len(devices), i) for i in devices]
    return lax.ppermute(block, axis, route)


def layer_norm(values):
    center = values - jnp.mean(values, -1, keepdims=True)
    return center * lax.rsqrt(jnp.mean(center * center, -1, keepdims=True) + norm_eps)


def rms_norm(values, norm_gain):
    return values * lax.rsqrt(jnp.mean(values * values, -1, keepdims=True) + norm_eps) * norm_gain


def _project_kernel(x_ref, w_ref, g_ref, o_ref, *, heads, head_dim, first):
    which = pl.program_id(0) + first
    mixed = jnp.dot(x_ref[...], w_ref[...], preferred_element_type=jnp.float32)
    gain = g_ref[pl.ds(which, 1), :]
    for h in range(heads):
        block = mixed[:, h * head_dim : (h + 1) * head_dim]
        normed = (
            block * lax.rsqrt(jnp.mean(block * block, -1, keepdims=True) + norm_eps) * gain
        )
        o_ref[:, h * head_dim : (h + 1) * head_dim] = jnp.where(
            which < 2, normed, block
        ).astype(o_ref.dtype)


def project(x, w, gains, head_dim, first, count):
    rows, width = x.shape
    local_width = w.shape[2]
    heads = local_width // head_dim
    kernel = functools.partial(_project_kernel, heads=heads, head_dim=head_dim, first=first)
    return pl.pallas_call(
        kernel,
        grid=(count,),
        in_specs=[
            pl.BlockSpec((rows, width), lambda c: (0, 0)),
            pl.BlockSpec((None, width, local_width), lambda c: (c + first, 0, 0)),
            pl.BlockSpec(gains.shape, lambda c: (0, 0)),
        ],
        out_specs=pl.BlockSpec((None, rows, local_width), lambda c: (c, 0, 0)),
        out_shape=jax.ShapeDtypeStruct((count, rows, local_width), jnp.bfloat16),
        compiler_params=pltpu.CompilerParams(vmem_limit_bytes=48 * 1024 * 1024),
    )(x, w, gains)


def _attend_kernel(*refs, scaling, sources):
    q_ref, o_ref = refs[0], refs[-1]
    pairs = refs[1:-1]

    def scores_of(keys):
        return lax.dot_general(
            q_ref[...], keys[...], (((1,), (1,)), ((), ())), preferred_element_type=jnp.float32
        ) * scaling

    scores = [scores_of(pairs[2 * n]) for n in range(sources)]
    row_max = jnp.max(scores[0], -1, keepdims=True)
    for block in scores[1:]:
        row_max = jnp.maximum(row_max, jnp.max(block, -1, keepdims=True))
    weights = [jnp.exp(block - row_max) for block in scores]
    row_sum = sum(jnp.sum(block, -1, keepdims=True) for block in weights)
    summed = sum(
        jnp.dot(block.astype(jnp.bfloat16), pairs[2 * n + 1][...], preferred_element_type=jnp.float32)
        for n, block in enumerate(weights)
    )
    o_ref[...] = (summed / row_sum).astype(o_ref.dtype)


def attend(queries, key_sources, head_dim, block_q=512):
    rows, width = queries.shape[1], queries.shape[2]
    heads = width // head_dim
    block_q = min(block_q, rows)
    kernel = functools.partial(
        _attend_kernel, scaling=head_dim ** (-0.5), sources=len(key_sources)
    )
    in_specs = [pl.BlockSpec((None, block_q, head_dim), lambda h, i: (0, i, h))]
    operands = [queries]
    for source, first in key_sources:
        extent = source.shape[1]
        for index in (first, first + 1):
            in_specs.append(
                pl.BlockSpec((None, extent, head_dim), lambda h, i, index=index: (index, 0, h))
            )
            operands.append(source)
    return pl.pallas_call(
        kernel,
        grid=(heads, rows // block_q),
        in_specs=in_specs,
        out_specs=pl.BlockSpec((block_q, head_dim), lambda h, i: (i, h)),
        out_shape=jax.ShapeDtypeStruct((rows, width), jnp.bfloat16),
        compiler_params=pltpu.CompilerParams(vmem_limit_bytes=48 * 1024 * 1024),
    )(*operands)


def _attend_own_kernel(q_ref, k_ref, v_ref, acc_ref, max_ref, sum_ref, *, scaling):
    scores = lax.dot_general(
        q_ref[...], k_ref[...], (((1,), (1,)), ((), ())), preferred_element_type=jnp.float32
    ) * scaling
    row_max = jnp.max(scores, -1, keepdims=True)
    weight = jnp.exp(scores - row_max)
    row_sum = jnp.sum(weight, -1, keepdims=True)
    acc_ref[...] = jnp.dot(
        weight.astype(jnp.bfloat16), v_ref[...], preferred_element_type=jnp.float32
    )
    max_ref[...] = jnp.broadcast_to(row_max, max_ref.shape)
    sum_ref[...] = jnp.broadcast_to(row_sum, sum_ref.shape)


def _attend_far_kernel(q_ref, k_ref, v_ref, acc_ref, max_ref, sum_ref, o_ref, *, scaling):
    scores = lax.dot_general(
        q_ref[...], k_ref[...], (((1,), (1,)), ((), ())), preferred_element_type=jnp.float32
    ) * scaling
    own_max = max_ref[:, :1]
    row_max = jnp.maximum(own_max, jnp.max(scores, -1, keepdims=True))
    rescale = jnp.exp(own_max - row_max)
    weight = jnp.exp(scores - row_max)
    row_sum = sum_ref[:, :1] * rescale + jnp.sum(weight, -1, keepdims=True)
    summed = acc_ref[...] * rescale + jnp.dot(
        weight.astype(jnp.bfloat16), v_ref[...], preferred_element_type=jnp.float32
    )
    o_ref[...] = (summed / row_sum).astype(o_ref.dtype)


def _attend_specs(queries, pairs, head_dim, block_q):
    keys = pairs.shape[1]
    return [
        pl.BlockSpec((None, block_q, head_dim), lambda h, i: (0, i, h)),
        pl.BlockSpec((None, keys, head_dim), lambda h, i: (0, 0, h)),
        pl.BlockSpec((None, keys, head_dim), lambda h, i: (1, 0, h)),
    ]


def attend_own(queries, pairs, head_dim, block_q=512):
    rows, width = queries.shape[1], queries.shape[2]
    heads = width // head_dim
    tile = pl.BlockSpec((block_q, head_dim), lambda h, i: (i, h))
    stats = jax.ShapeDtypeStruct((rows, width), jnp.float32)
    return pl.pallas_call(
        functools.partial(_attend_own_kernel, scaling=head_dim ** (-0.5)),
        grid=(heads, rows // block_q),
        in_specs=_attend_specs(queries, pairs, head_dim, block_q),
        out_specs=[tile, tile, tile],
        out_shape=[stats, stats, stats],
        compiler_params=pltpu.CompilerParams(vmem_limit_bytes=48 * 1024 * 1024),
    )(queries, pairs, pairs)


def attend_far(queries, pairs, partial, head_dim, block_q=512):
    rows, width = queries.shape[1], queries.shape[2]
    heads = width // head_dim
    tile = pl.BlockSpec((block_q, head_dim), lambda h, i: (i, h))
    return pl.pallas_call(
        functools.partial(_attend_far_kernel, scaling=head_dim ** (-0.5)),
        grid=(heads, rows // block_q),
        in_specs=_attend_specs(queries, pairs, head_dim, block_q) + [tile, tile, tile],
        out_specs=tile,
        out_shape=jax.ShapeDtypeStruct((rows, width), jnp.bfloat16),
        compiler_params=pltpu.CompilerParams(vmem_limit_bytes=48 * 1024 * 1024),
    )(queries, pairs, pairs, *partial)


def body(inputs, modulation, w_qkv, w_attn_out, qk_gain, final_mod, w_final, w_embed, latent):
    head_dim = qk_gain.shape[2]
    x_rows = inputs[0]
    samples, tokens_local, width = x_rows.shape
    n_seq = lax.axis_size("seq")
    parts = n_seq // samples
    mod_rows = modulation[0]
    x_float = x_rows.astype(jnp.float32)
    x_mod = (
        layer_norm(x_float) * (1.0 + mod_rows[:, 1, None, :]) + mod_rows[:, 0, None, :]
    ).astype(jnp.bfloat16)
    weights = jnp.transpose(w_qkv[0], (1, 0, 2))
    local_width = weights.shape[2]
    norm_gains = qk_gain[0]
    gains = jnp.concatenate([norm_gains, jnp.ones_like(norm_gains[:1])], 0)
    ring = n_seq // parts
    groups = [list(range(p * ring, (p + 1) * ring)) for p in range(parts)]
    partner = [(i, (i + ring) % n_seq) for i in range(n_seq)]
    x_clip = lax.all_to_all(x_mod, "seq", 0, 0, tiled=True, axis_index_groups=groups)
    x_group = lax.all_gather(x_clip, "tp", axis=0, tiled=False)
    n_tp, n_src = x_group.shape[0], x_group.shape[1]
    rows = n_tp * n_src * tokens_local
    x_group = x_group.reshape(rows, width)
    pairs = project(x_group, weights, gains, head_dim, 1, 2)
    other = lax.ppermute(pairs, "seq", partner)
    queried = project(x_group, weights, gains, head_dim, 0, 1)
    partial = attend_own(queried, pairs, head_dim)
    attended = attend_far(queried, other, partial, head_dim)
    partial_out = jnp.einsum(
        "re,ed->rd", attended, w_attn_out[0], preferred_element_type=jnp.float32
    )
    branch_clip = lax.psum_scatter(
        partial_out.astype(jnp.bfloat16).reshape(n_tp, n_src * tokens_local, width),
        "tp",
        scatter_dimension=0,
        tiled=True,
    ).reshape(n_src, tokens_local, width)
    branch = (
        lax.all_to_all(branch_clip, "seq", 0, 0, tiled=True, axis_index_groups=groups)
        .reshape(samples, tokens_local, width)
        .astype(jnp.float32)
    )
    output = (x_float + mod_rows[:, 2, None, :] * branch).astype(jnp.bfloat16)
    final_in = (
        layer_norm(output.astype(jnp.float32)) * (1.0 + final_mod[:, 1, None, :])
        + final_mod[:, 0, None, :]
    ).astype(jnp.bfloat16)
    velocity = jnp.einsum("srd,dc->scr", final_in, w_final, preferred_element_type=jnp.float32)
    advanced = latent + step_size * velocity
    last_comp = lax.axis_size("comp") - 1
    position = lax.axis_index("comp")
    shared = jnp.stack([velocity, advanced]).astype(jnp.bfloat16)
    embedded = jnp.einsum(
        "scr,cd->srd", advanced.astype(jnp.bfloat16), w_embed, preferred_element_type=jnp.float32
    ).astype(jnp.bfloat16)
    sending = jnp.where(position == last_comp, embedded, output)
    packed = jnp.concatenate([sending.reshape(-1), shared.reshape(-1)])
    arrived = shifted(packed, "comp", 1)
    handed = arrived[: sending.size].reshape(sending.shape)
    from_last = arrived[sending.size :].reshape(shared.shape)
    shared = jnp.where(position == last_comp, shared, from_last).astype(jnp.float32)
    return (handed[None], shared[0], shared[1])


def solution(mesh):
    in_specs = (
        P("comp", None, ("seq", "tp"), None),
        P("comp", None, None, None),
        P("comp", None, None, "tp"),
        P("comp", "tp", None),
        P("comp", None, None),
        P(),
        P(),
        P(),
        P(None, None, ("seq", "tp")),
    )
    out_specs = (
        P("comp", None, ("seq", "tp"), None),
        P(None, None, ("seq", "tp")),
        P(None, None, ("seq", "tp")),
    )
    return jax.shard_map(body, mesh=mesh, in_specs=in_specs, out_specs=out_specs, check_vma=False)
```

```python
import jax
import jax.numpy as jnp
from jax import lax
import functools
from jax.experimental import pallas as pl
from jax.experimental.pallas import tpu as pltpu
from jax.sharding import PartitionSpec as P


step_size = 0.02
norm_eps = 1e-06


def broadcast(block, axis, owner):
    block = jnp.where(lax.axis_index(axis) == owner, block, jnp.zeros_like(block))
    return lax.psum(block, axis)


def shifted(block, axis, distance):
    devices = range(lax.axis_size(axis))
    route = [((i - distance) % len(devices), i) for i in devices]
    return lax.ppermute(block, axis, route)


def layer_norm(values):
    center = values - jnp.mean(values, -1, keepdims=True)
    return center * lax.rsqrt(jnp.mean(center * center, -1, keepdims=True) + norm_eps)


def rms_norm(values, norm_gain):
    return values * lax.rsqrt(jnp.mean(values * values, -1, keepdims=True) + norm_eps) * norm_gain


def _project_kernel(x_ref, w_ref, g_ref, o_ref, *, heads, head_dim, first):
    which = pl.program_id(0) + first
    mixed = jnp.dot(x_ref[...], w_ref[...], preferred_element_type=jnp.float32)
    gain = g_ref[pl.ds(which, 1), :]
    for h in range(heads):
        block = mixed[:, h * head_dim : (h + 1) * head_dim]
        normed = (
            block * lax.rsqrt(jnp.mean(block * block, -1, keepdims=True) + norm_eps) * gain
        )
        o_ref[:, h * head_dim : (h + 1) * head_dim] = jnp.where(
            which < 2, normed, block
        ).astype(o_ref.dtype)


def project(x, w, gains, head_dim, first, count):
    rows, width = x.shape
    local_width = w.shape[2]
    heads = local_width // head_dim
    kernel = functools.partial(_project_kernel, heads=heads, head_dim=head_dim, first=first)
    return pl.pallas_call(
        kernel,
        grid=(count,),
        in_specs=[
            pl.BlockSpec((rows, width), lambda c: (0, 0)),
            pl.BlockSpec((None, width, local_width), lambda c: (c + first, 0, 0)),
            pl.BlockSpec(gains.shape, lambda c: (0, 0)),
        ],
        out_specs=pl.BlockSpec((None, rows, local_width), lambda c: (c, 0, 0)),
        out_shape=jax.ShapeDtypeStruct((count, rows, local_width), jnp.bfloat16),
        compiler_params=pltpu.CompilerParams(vmem_limit_bytes=48 * 1024 * 1024),
    )(x, w, gains)


def _attend_kernel(*refs, scaling, sources):
    q_ref, o_ref = refs[0], refs[-1]
    pairs = refs[1:-1]

    def scores_of(keys):
        return lax.dot_general(
            q_ref[...], keys[...], (((1,), (1,)), ((), ())), preferred_element_type=jnp.float32
        ) * scaling

    scores = [scores_of(pairs[2 * n]) for n in range(sources)]
    row_max = jnp.max(scores[0], -1, keepdims=True)
    for block in scores[1:]:
        row_max = jnp.maximum(row_max, jnp.max(block, -1, keepdims=True))
    weights = [jnp.exp(block - row_max) for block in scores]
    row_sum = sum(jnp.sum(block, -1, keepdims=True) for block in weights)
    summed = sum(
        jnp.dot(block.astype(jnp.bfloat16), pairs[2 * n + 1][...], preferred_element_type=jnp.float32)
        for n, block in enumerate(weights)
    )
    o_ref[...] = (summed / row_sum).astype(o_ref.dtype)


def attend(queries, key_sources, head_dim, block_q=512):
    rows, width = queries.shape[1], queries.shape[2]
    heads = width // head_dim
    block_q = min(block_q, rows)
    kernel = functools.partial(
        _attend_kernel, scaling=head_dim ** (-0.5), sources=len(key_sources)
    )
    in_specs = [pl.BlockSpec((None, block_q, head_dim), lambda h, i: (0, i, h))]
    operands = [queries]
    for source, first in key_sources:
        extent = source.shape[1]
        for index in (first, first + 1):
            in_specs.append(
                pl.BlockSpec((None, extent, head_dim), lambda h, i, index=index: (index, 0, h))
            )
            operands.append(source)
    return pl.pallas_call(
        kernel,
        grid=(heads, rows // block_q),
        in_specs=in_specs,
        out_specs=pl.BlockSpec((block_q, head_dim), lambda h, i: (i, h)),
        out_shape=jax.ShapeDtypeStruct((rows, width), jnp.bfloat16),
        compiler_params=pltpu.CompilerParams(vmem_limit_bytes=48 * 1024 * 1024),
    )(*operands)


def _attend_own_kernel(q_ref, k_ref, v_ref, acc_ref, max_ref, sum_ref, *, scaling):
    scores = lax.dot_general(
        q_ref[...], k_ref[...], (((1,), (1,)), ((), ())), preferred_element_type=jnp.float32
    ) * scaling
    row_max = jnp.max(scores, -1, keepdims=True)
    weight = jnp.exp(scores - row_max)
    row_sum = jnp.sum(weight, -1, keepdims=True)
    acc_ref[...] = jnp.dot(
        weight.astype(jnp.bfloat16), v_ref[...], preferred_element_type=jnp.float32
    )
    max_ref[...] = jnp.broadcast_to(row_max, max_ref.shape)
    sum_ref[...] = jnp.broadcast_to(row_sum, sum_ref.shape)


def _attend_far_kernel(q_ref, k_ref, v_ref, acc_ref, max_ref, sum_ref, o_ref, *, scaling):
    scores = lax.dot_general(
        q_ref[...], k_ref[...], (((1,), (1,)), ((), ())), preferred_element_type=jnp.float32
    ) * scaling
    own_max = max_ref[:, :1]
    row_max = jnp.maximum(own_max, jnp.max(scores, -1, keepdims=True))
    rescale = jnp.exp(own_max - row_max)
    weight = jnp.exp(scores - row_max)
    row_sum = sum_ref[:, :1] * rescale + jnp.sum(weight, -1, keepdims=True)
    summed = acc_ref[...] * rescale + jnp.dot(
        weight.astype(jnp.bfloat16), v_ref[...], preferred_element_type=jnp.float32
    )
    o_ref[...] = (summed / row_sum).astype(o_ref.dtype)


def _attend_specs(queries, pairs, head_dim, block_q):
    keys = pairs.shape[1]
    return [
        pl.BlockSpec((None, block_q, head_dim), lambda h, i: (0, i, h)),
        pl.BlockSpec((None, keys, head_dim), lambda h, i: (0, 0, h)),
        pl.BlockSpec((None, keys, head_dim), lambda h, i: (1, 0, h)),
    ]


def attend_own(queries, pairs, head_dim, block_q=512):
    rows, width = queries.shape[1], queries.shape[2]
    heads = width // head_dim
    tile = pl.BlockSpec((block_q, head_dim), lambda h, i: (i, h))
    stats = jax.ShapeDtypeStruct((rows, width), jnp.float32)
    return pl.pallas_call(
        functools.partial(_attend_own_kernel, scaling=head_dim ** (-0.5)),
        grid=(heads, rows // block_q),
        in_specs=_attend_specs(queries, pairs, head_dim, block_q),
        out_specs=[tile, tile, tile],
        out_shape=[stats, stats, stats],
        compiler_params=pltpu.CompilerParams(vmem_limit_bytes=48 * 1024 * 1024),
    )(queries, pairs, pairs)


def attend_far(queries, pairs, partial, head_dim, block_q=512):
    rows, width = queries.shape[1], queries.shape[2]
    heads = width // head_dim
    tile = pl.BlockSpec((block_q, head_dim), lambda h, i: (i, h))
    return pl.pallas_call(
        functools.partial(_attend_far_kernel, scaling=head_dim ** (-0.5)),
        grid=(heads, rows // block_q),
        in_specs=_attend_specs(queries, pairs, head_dim, block_q) + [tile, tile, tile],
        out_specs=tile,
        out_shape=jax.ShapeDtypeStruct((rows, width), jnp.bfloat16),
        compiler_params=pltpu.CompilerParams(vmem_limit_bytes=48 * 1024 * 1024),
    )(queries, pairs, pairs, *partial)


def gather_by_distance(block, axis):
    count = lax.axis_size(axis)
    received = [block]
    for step in range(1, count):
        route = [(i, (i + step) % count) for i in range(count)]
        received.append(lax.ppermute(block, axis, route))
    return jnp.stack(received)


def scatter_by_distance(blocks, axis):
    count = lax.axis_size(axis)
    total = blocks[0].astype(jnp.float32)
    for step in range(1, count):
        route = [(i, (i + step) % count) for i in range(count)]
        total = total + lax.ppermute(blocks[count - step], axis, route).astype(jnp.float32)
    return total


def body(inputs, modulation, w_qkv, w_attn_out, qk_gain, final_mod, w_final, w_embed, latent):
    head_dim = qk_gain.shape[2]
    x_rows = inputs[0]
    samples, tokens_local, width = x_rows.shape
    n_seq = lax.axis_size("seq")
    parts = n_seq // samples
    mod_rows = modulation[0]
    x_float = x_rows.astype(jnp.float32)
    x_mod = (
        layer_norm(x_float) * (1.0 + mod_rows[:, 1, None, :]) + mod_rows[:, 0, None, :]
    ).astype(jnp.bfloat16)
    weights = jnp.transpose(w_qkv[0], (1, 0, 2))
    local_width = weights.shape[2]
    norm_gains = qk_gain[0]
    gains = jnp.concatenate([norm_gains, jnp.ones_like(norm_gains[:1])], 0)
    ring = n_seq // parts
    groups = [list(range(p * ring, (p + 1) * ring)) for p in range(parts)]
    partner = [(i, (i + ring) % n_seq) for i in range(n_seq)]
    x_clip = lax.all_to_all(x_mod, "seq", 0, 0, tiled=True, axis_index_groups=groups)
    x_group = gather_by_distance(x_clip, "tp")
    n_tp, n_src = x_group.shape[0], x_group.shape[1]
    rows = n_tp * n_src * tokens_local
    x_group = x_group.reshape(rows, width)
    pairs = project(x_group, weights, gains, head_dim, 1, 2)
    other = lax.ppermute(pairs, "seq", partner)
    queried = project(x_group, weights, gains, head_dim, 0, 1)
    partial = attend_own(queried, pairs, head_dim)
    attended = attend_far(queried, other, partial, head_dim)
    partial_out = jnp.einsum(
        "re,ed->rd", attended, w_attn_out[0], preferred_element_type=jnp.float32
    )
    branch_clip = scatter_by_distance(
        partial_out.astype(jnp.bfloat16).reshape(n_tp, n_src * tokens_local, width), "tp"
    ).astype(jnp.bfloat16).reshape(n_src, tokens_local, width)
    branch = (
        lax.all_to_all(branch_clip, "seq", 0, 0, tiled=True, axis_index_groups=groups)
        .reshape(samples, tokens_local, width)
        .astype(jnp.float32)
    )
    output = (x_float + mod_rows[:, 2, None, :] * branch).astype(jnp.bfloat16)
    final_in = (
        layer_norm(output.astype(jnp.float32)) * (1.0 + final_mod[:, 1, None, :])
        + final_mod[:, 0, None, :]
    ).astype(jnp.bfloat16)
    velocity = jnp.einsum("srd,dc->scr", final_in, w_final, preferred_element_type=jnp.float32)
    advanced = latent + step_size * velocity
    last_comp = lax.axis_size("comp") - 1
    position = lax.axis_index("comp")
    shared = jnp.stack([velocity, advanced]).astype(jnp.bfloat16)
    embedded = jnp.einsum(
        "scr,cd->srd", advanced.astype(jnp.bfloat16), w_embed, preferred_element_type=jnp.float32
    ).astype(jnp.bfloat16)
    sending = jnp.where(position == last_comp, embedded, output)
    packed = jnp.concatenate([sending.reshape(-1), shared.reshape(-1)])
    arrived = shifted(packed, "comp", 1)
    handed = arrived[: sending.size].reshape(sending.shape)
    from_last = arrived[sending.size :].reshape(shared.shape)
    shared = jnp.where(position == last_comp, shared, from_last).astype(jnp.float32)
    return (handed[None], shared[0], shared[1])


def solution(mesh):
    in_specs = (
        P("comp", None, ("seq", "tp"), None),
        P("comp", None, None, None),
        P("comp", None, None, "tp"),
        P("comp", "tp", None),
        P("comp", None, None),
        P(),
        P(),
        P(),
        P(None, None, ("seq", "tp")),
    )
    out_specs = (
        P("comp", None, ("seq", "tp"), None),
        P(None, None, ("seq", "tp")),
        P(None, None, ("seq", "tp")),
    )
    return jax.shard_map(body, mesh=mesh, in_specs=in_specs, out_specs=out_specs, check_vma=False)
```

```python
import jax
import jax.numpy as jnp
from jax import lax
import functools
from jax.experimental import pallas as pl
from jax.experimental.pallas import tpu as pltpu
from jax.sharding import PartitionSpec as P


step_size = 0.02
norm_eps = 1e-06


def broadcast(block, axis, owner):
    block = jnp.where(lax.axis_index(axis) == owner, block, jnp.zeros_like(block))
    return lax.psum(block, axis)


def shifted(block, axis, distance):
    devices = range(lax.axis_size(axis))
    route = [((i - distance) % len(devices), i) for i in devices]
    return lax.ppermute(block, axis, route)


def layer_norm(values):
    center = values - jnp.mean(values, -1, keepdims=True)
    return center * lax.rsqrt(jnp.mean(center * center, -1, keepdims=True) + norm_eps)


def rms_norm(values, norm_gain):
    return values * lax.rsqrt(jnp.mean(values * values, -1, keepdims=True) + norm_eps) * norm_gain


def _project_kernel(x_ref, w_ref, g_ref, o_ref, *, heads, head_dim, first):
    which = pl.program_id(0) + first
    mixed = jnp.dot(x_ref[...], w_ref[...], preferred_element_type=jnp.float32)
    gain = g_ref[pl.ds(which, 1), :]
    for h in range(heads):
        block = mixed[:, h * head_dim : (h + 1) * head_dim]
        normed = (
            block * lax.rsqrt(jnp.mean(block * block, -1, keepdims=True) + norm_eps) * gain
        )
        o_ref[:, h * head_dim : (h + 1) * head_dim] = jnp.where(
            which < 2, normed, block
        ).astype(o_ref.dtype)


def project(x, w, gains, head_dim, first, count):
    rows, width = x.shape
    local_width = w.shape[2]
    heads = local_width // head_dim
    kernel = functools.partial(_project_kernel, heads=heads, head_dim=head_dim, first=first)
    return pl.pallas_call(
        kernel,
        grid=(count,),
        in_specs=[
            pl.BlockSpec((rows, width), lambda c: (0, 0)),
            pl.BlockSpec((None, width, local_width), lambda c: (c + first, 0, 0)),
            pl.BlockSpec(gains.shape, lambda c: (0, 0)),
        ],
        out_specs=pl.BlockSpec((None, rows, local_width), lambda c: (c, 0, 0)),
        out_shape=jax.ShapeDtypeStruct((count, rows, local_width), jnp.bfloat16),
        compiler_params=pltpu.CompilerParams(vmem_limit_bytes=48 * 1024 * 1024),
    )(x, w, gains)


def _attend_kernel(*refs, scaling, sources):
    q_ref, o_ref = refs[0], refs[-1]
    pairs = refs[1:-1]

    def scores_of(keys):
        return lax.dot_general(
            q_ref[...], keys[...], (((1,), (1,)), ((), ())), preferred_element_type=jnp.float32
        ) * scaling

    scores = [scores_of(pairs[2 * n]) for n in range(sources)]
    row_max = jnp.max(scores[0], -1, keepdims=True)
    for block in scores[1:]:
        row_max = jnp.maximum(row_max, jnp.max(block, -1, keepdims=True))
    weights = [jnp.exp(block - row_max) for block in scores]
    row_sum = sum(jnp.sum(block, -1, keepdims=True) for block in weights)
    summed = sum(
        jnp.dot(block.astype(jnp.bfloat16), pairs[2 * n + 1][...], preferred_element_type=jnp.float32)
        for n, block in enumerate(weights)
    )
    o_ref[...] = (summed / row_sum).astype(o_ref.dtype)


def attend(queries, key_sources, head_dim, block_q=512):
    rows, width = queries.shape[1], queries.shape[2]
    heads = width // head_dim
    block_q = min(block_q, rows)
    kernel = functools.partial(
        _attend_kernel, scaling=head_dim ** (-0.5), sources=len(key_sources)
    )
    in_specs = [pl.BlockSpec((None, block_q, head_dim), lambda h, i: (0, i, h))]
    operands = [queries]
    for source, first in key_sources:
        extent = source.shape[1]
        for index in (first, first + 1):
            in_specs.append(
                pl.BlockSpec((None, extent, head_dim), lambda h, i, index=index: (index, 0, h))
            )
            operands.append(source)
    return pl.pallas_call(
        kernel,
        grid=(heads, rows // block_q),
        in_specs=in_specs,
        out_specs=pl.BlockSpec((block_q, head_dim), lambda h, i: (i, h)),
        out_shape=jax.ShapeDtypeStruct((rows, width), jnp.bfloat16),
        compiler_params=pltpu.CompilerParams(vmem_limit_bytes=48 * 1024 * 1024),
    )(*operands)


def _attend_own_kernel(q_ref, k_ref, v_ref, acc_ref, max_ref, sum_ref, *, scaling):
    scores = lax.dot_general(
        q_ref[...], k_ref[...], (((1,), (1,)), ((), ())), preferred_element_type=jnp.float32
    ) * scaling
    row_max = jnp.max(scores, -1, keepdims=True)
    weight = jnp.exp(scores - row_max)
    row_sum = jnp.sum(weight, -1, keepdims=True)
    acc_ref[...] = jnp.dot(
        weight.astype(jnp.bfloat16), v_ref[...], preferred_element_type=jnp.float32
    )
    max_ref[...] = jnp.broadcast_to(row_max, max_ref.shape)
    sum_ref[...] = jnp.broadcast_to(row_sum, sum_ref.shape)


def _attend_far_kernel(q_ref, k_ref, v_ref, acc_ref, max_ref, sum_ref, o_ref, *, scaling):
    scores = lax.dot_general(
        q_ref[...], k_ref[...], (((1,), (1,)), ((), ())), preferred_element_type=jnp.float32
    ) * scaling
    own_max = max_ref[:, :1]
    row_max = jnp.maximum(own_max, jnp.max(scores, -1, keepdims=True))
    rescale = jnp.exp(own_max - row_max)
    weight = jnp.exp(scores - row_max)
    row_sum = sum_ref[:, :1] * rescale + jnp.sum(weight, -1, keepdims=True)
    summed = acc_ref[...] * rescale + jnp.dot(
        weight.astype(jnp.bfloat16), v_ref[...], preferred_element_type=jnp.float32
    )
    o_ref[...] = (summed / row_sum).astype(o_ref.dtype)


def _attend_specs(queries, pairs, head_dim, block_q):
    keys = pairs.shape[1]
    return [
        pl.BlockSpec((None, block_q, head_dim), lambda h, i: (0, i, h)),
        pl.BlockSpec((None, keys, head_dim), lambda h, i: (0, 0, h)),
        pl.BlockSpec((None, keys, head_dim), lambda h, i: (1, 0, h)),
    ]


def attend_own(queries, pairs, head_dim, block_q=512):
    rows, width = queries.shape[1], queries.shape[2]
    heads = width // head_dim
    tile = pl.BlockSpec((block_q, head_dim), lambda h, i: (i, h))
    stats = jax.ShapeDtypeStruct((rows, width), jnp.float32)
    return pl.pallas_call(
        functools.partial(_attend_own_kernel, scaling=head_dim ** (-0.5)),
        grid=(heads, rows // block_q),
        in_specs=_attend_specs(queries, pairs, head_dim, block_q),
        out_specs=[tile, tile, tile],
        out_shape=[stats, stats, stats],
        compiler_params=pltpu.CompilerParams(vmem_limit_bytes=48 * 1024 * 1024),
    )(queries, pairs, pairs)


def attend_far(queries, pairs, partial, head_dim, block_q=512):
    rows, width = queries.shape[1], queries.shape[2]
    heads = width // head_dim
    tile = pl.BlockSpec((block_q, head_dim), lambda h, i: (i, h))
    return pl.pallas_call(
        functools.partial(_attend_far_kernel, scaling=head_dim ** (-0.5)),
        grid=(heads, rows // block_q),
        in_specs=_attend_specs(queries, pairs, head_dim, block_q) + [tile, tile, tile],
        out_specs=tile,
        out_shape=jax.ShapeDtypeStruct((rows, width), jnp.bfloat16),
        compiler_params=pltpu.CompilerParams(vmem_limit_bytes=48 * 1024 * 1024),
    )(queries, pairs, pairs, *partial)


def gather_by_distance(block, axis):
    count = lax.axis_size(axis)
    received = [block]
    for step in range(1, count):
        route = [(i, (i + step) % count) for i in range(count)]
        received.append(lax.ppermute(block, axis, route))
    return received


def scatter_by_distance(blocks, axis):
    count = lax.axis_size(axis)
    total = blocks[0].astype(jnp.float32)
    for step in range(1, count):
        route = [(i, (i + step) % count) for i in range(count)]
        total = total + lax.ppermute(blocks[count - step], axis, route).astype(jnp.float32)
    return total


def body(inputs, modulation, w_qkv, w_attn_out, qk_gain, final_mod, w_final, w_embed, latent):
    head_dim = qk_gain.shape[2]
    x_rows = inputs[0]
    samples, tokens_local, width = x_rows.shape
    n_seq = lax.axis_size("seq")
    parts = n_seq // samples
    mod_rows = modulation[0]
    x_float = x_rows.astype(jnp.float32)
    x_mod = (
        layer_norm(x_float) * (1.0 + mod_rows[:, 1, None, :]) + mod_rows[:, 0, None, :]
    ).astype(jnp.bfloat16)
    weights = jnp.transpose(w_qkv[0], (1, 0, 2))
    local_width = weights.shape[2]
    norm_gains = qk_gain[0]
    gains = jnp.concatenate([norm_gains, jnp.ones_like(norm_gains[:1])], 0)
    ring = n_seq // parts
    groups = [list(range(p * ring, (p + 1) * ring)) for p in range(parts)]
    partner = [(i, (i + ring) % n_seq) for i in range(n_seq)]
    x_clip = lax.all_to_all(x_mod, "seq", 0, 0, tiled=True, axis_index_groups=groups)
    received = gather_by_distance(x_clip, "tp")
    n_tp, n_src = len(received), x_clip.shape[0]
    rows = n_tp * n_src * tokens_local
    pairs = jnp.concatenate(
        [
            project(block.reshape(-1, width), weights, gains, head_dim, 1, 2)
            for block in received
        ],
        1,
    )
    other = lax.ppermute(pairs, "seq", partner)
    x_group = jnp.stack(received).reshape(rows, width)
    queried = project(x_group, weights, gains, head_dim, 0, 1)
    partial = attend_own(queried, pairs, head_dim)
    attended = attend_far(queried, other, partial, head_dim)
    partial_out = jnp.einsum(
        "re,ed->rd", attended, w_attn_out[0], preferred_element_type=jnp.float32
    )
    branch_clip = scatter_by_distance(
        partial_out.astype(jnp.bfloat16).reshape(n_tp, n_src * tokens_local, width), "tp"
    ).astype(jnp.bfloat16).reshape(n_src, tokens_local, width)
    branch = (
        lax.all_to_all(branch_clip, "seq", 0, 0, tiled=True, axis_index_groups=groups)
        .reshape(samples, tokens_local, width)
        .astype(jnp.float32)
    )
    output = (x_float + mod_rows[:, 2, None, :] * branch).astype(jnp.bfloat16)
    final_in = (
        layer_norm(output.astype(jnp.float32)) * (1.0 + final_mod[:, 1, None, :])
        + final_mod[:, 0, None, :]
    ).astype(jnp.bfloat16)
    velocity = jnp.einsum("srd,dc->scr", final_in, w_final, preferred_element_type=jnp.float32)
    advanced = latent + step_size * velocity
    last_comp = lax.axis_size("comp") - 1
    position = lax.axis_index("comp")
    shared = jnp.stack([velocity, advanced]).astype(jnp.bfloat16)
    embedded = jnp.einsum(
        "scr,cd->srd", advanced.astype(jnp.bfloat16), w_embed, preferred_element_type=jnp.float32
    ).astype(jnp.bfloat16)
    sending = jnp.where(position == last_comp, embedded, output)
    packed = jnp.concatenate([sending.reshape(-1), shared.reshape(-1)])
    arrived = shifted(packed, "comp", 1)
    handed = arrived[: sending.size].reshape(sending.shape)
    from_last = arrived[sending.size :].reshape(shared.shape)
    shared = jnp.where(position == last_comp, shared, from_last).astype(jnp.float32)
    return (handed[None], shared[0], shared[1])


def solution(mesh):
    in_specs = (
        P("comp", None, ("seq", "tp"), None),
        P("comp", None, None, None),
        P("comp", None, None, "tp"),
        P("comp", "tp", None),
        P("comp", None, None),
        P(),
        P(),
        P(),
        P(None, None, ("seq", "tp")),
    )
    out_specs = (
        P("comp", None, ("seq", "tp"), None),
        P(None, None, ("seq", "tp")),
        P(None, None, ("seq", "tp")),
    )
    return jax.shard_map(body, mesh=mesh, in_specs=in_specs, out_specs=out_specs, check_vma=False)
```

```python
import jax
import jax.numpy as jnp
from jax import lax
import functools
from jax.experimental import pallas as pl
from jax.experimental.pallas import tpu as pltpu
from jax.sharding import PartitionSpec as P


step_size = 0.02
norm_eps = 1e-06


def broadcast(block, axis, owner):
    block = jnp.where(lax.axis_index(axis) == owner, block, jnp.zeros_like(block))
    return lax.psum(block, axis)


def shifted(block, axis, distance):
    devices = range(lax.axis_size(axis))
    route = [((i - distance) % len(devices), i) for i in devices]
    return lax.ppermute(block, axis, route)


def layer_norm(values):
    center = values - jnp.mean(values, -1, keepdims=True)
    return center * lax.rsqrt(jnp.mean(center * center, -1, keepdims=True) + norm_eps)


def rms_norm(values, norm_gain):
    return values * lax.rsqrt(jnp.mean(values * values, -1, keepdims=True) + norm_eps) * norm_gain


def _project_kernel(x_ref, w_ref, g_ref, o_ref, *, heads, head_dim, first):
    which = pl.program_id(0) + first
    mixed = jnp.dot(x_ref[...], w_ref[...], preferred_element_type=jnp.float32)
    gain = g_ref[pl.ds(which, 1), :]
    for h in range(heads):
        block = mixed[:, h * head_dim : (h + 1) * head_dim]
        normed = (
            block * lax.rsqrt(jnp.mean(block * block, -1, keepdims=True) + norm_eps) * gain
        )
        o_ref[:, h * head_dim : (h + 1) * head_dim] = jnp.where(
            which < 2, normed, block
        ).astype(o_ref.dtype)


def project(x, w, gains, head_dim, first, count):
    rows, width = x.shape
    local_width = w.shape[2]
    heads = local_width // head_dim
    kernel = functools.partial(_project_kernel, heads=heads, head_dim=head_dim, first=first)
    return pl.pallas_call(
        kernel,
        grid=(count,),
        in_specs=[
            pl.BlockSpec((rows, width), lambda c: (0, 0)),
            pl.BlockSpec((None, width, local_width), lambda c: (c + first, 0, 0)),
            pl.BlockSpec(gains.shape, lambda c: (0, 0)),
        ],
        out_specs=pl.BlockSpec((None, rows, local_width), lambda c: (c, 0, 0)),
        out_shape=jax.ShapeDtypeStruct((count, rows, local_width), jnp.bfloat16),
        compiler_params=pltpu.CompilerParams(vmem_limit_bytes=48 * 1024 * 1024),
    )(x, w, gains)


def _attend_kernel(*refs, scaling, sources):
    q_ref, o_ref = refs[0], refs[-1]
    pairs = refs[1:-1]

    def scores_of(keys):
        return lax.dot_general(
            q_ref[...], keys[...], (((1,), (1,)), ((), ())), preferred_element_type=jnp.float32
        ) * scaling

    scores = [scores_of(pairs[2 * n]) for n in range(sources)]
    row_max = jnp.max(scores[0], -1, keepdims=True)
    for block in scores[1:]:
        row_max = jnp.maximum(row_max, jnp.max(block, -1, keepdims=True))
    weights = [jnp.exp(block - row_max) for block in scores]
    row_sum = sum(jnp.sum(block, -1, keepdims=True) for block in weights)
    summed = sum(
        jnp.dot(block.astype(jnp.bfloat16), pairs[2 * n + 1][...], preferred_element_type=jnp.float32)
        for n, block in enumerate(weights)
    )
    o_ref[...] = (summed / row_sum).astype(o_ref.dtype)


def attend(queries, key_sources, head_dim, block_q=512):
    rows, width = queries.shape[1], queries.shape[2]
    heads = width // head_dim
    block_q = min(block_q, rows)
    kernel = functools.partial(
        _attend_kernel, scaling=head_dim ** (-0.5), sources=len(key_sources)
    )
    in_specs = [pl.BlockSpec((None, block_q, head_dim), lambda h, i: (0, i, h))]
    operands = [queries]
    for source, first in key_sources:
        extent = source.shape[1]
        for index in (first, first + 1):
            in_specs.append(
                pl.BlockSpec((None, extent, head_dim), lambda h, i, index=index: (index, 0, h))
            )
            operands.append(source)
    return pl.pallas_call(
        kernel,
        grid=(heads, rows // block_q),
        in_specs=in_specs,
        out_specs=pl.BlockSpec((block_q, head_dim), lambda h, i: (i, h)),
        out_shape=jax.ShapeDtypeStruct((rows, width), jnp.bfloat16),
        compiler_params=pltpu.CompilerParams(vmem_limit_bytes=48 * 1024 * 1024),
    )(*operands)


def _attend_own_kernel(q_ref, k_ref, v_ref, acc_ref, max_ref, sum_ref, *, scaling):
    scores = lax.dot_general(
        q_ref[...], k_ref[...], (((1,), (1,)), ((), ())), preferred_element_type=jnp.float32
    ) * scaling
    row_max = jnp.max(scores, -1, keepdims=True)
    weight = jnp.exp(scores - row_max)
    row_sum = jnp.sum(weight, -1, keepdims=True)
    acc_ref[...] = jnp.dot(
        weight.astype(jnp.bfloat16), v_ref[...], preferred_element_type=jnp.float32
    )
    max_ref[...] = jnp.broadcast_to(row_max, max_ref.shape)
    sum_ref[...] = jnp.broadcast_to(row_sum, sum_ref.shape)


def _attend_far_kernel(q_ref, k_ref, v_ref, acc_ref, max_ref, sum_ref, o_ref, *, scaling):
    scores = lax.dot_general(
        q_ref[...], k_ref[...], (((1,), (1,)), ((), ())), preferred_element_type=jnp.float32
    ) * scaling
    own_max = max_ref[:, :1]
    row_max = jnp.maximum(own_max, jnp.max(scores, -1, keepdims=True))
    rescale = jnp.exp(own_max - row_max)
    weight = jnp.exp(scores - row_max)
    row_sum = sum_ref[:, :1] * rescale + jnp.sum(weight, -1, keepdims=True)
    summed = acc_ref[...] * rescale + jnp.dot(
        weight.astype(jnp.bfloat16), v_ref[...], preferred_element_type=jnp.float32
    )
    o_ref[...] = (summed / row_sum).astype(o_ref.dtype)


def _attend_specs(queries, pairs, head_dim, block_q):
    keys = pairs.shape[1]
    return [
        pl.BlockSpec((None, block_q, head_dim), lambda h, i: (0, i, h)),
        pl.BlockSpec((None, keys, head_dim), lambda h, i: (0, 0, h)),
        pl.BlockSpec((None, keys, head_dim), lambda h, i: (1, 0, h)),
    ]


def attend_own(queries, pairs, head_dim, block_q=512):
    rows, width = queries.shape[1], queries.shape[2]
    heads = width // head_dim
    tile = pl.BlockSpec((block_q, head_dim), lambda h, i: (i, h))
    stats = jax.ShapeDtypeStruct((rows, width), jnp.float32)
    return pl.pallas_call(
        functools.partial(_attend_own_kernel, scaling=head_dim ** (-0.5)),
        grid=(heads, rows // block_q),
        in_specs=_attend_specs(queries, pairs, head_dim, block_q),
        out_specs=[tile, tile, tile],
        out_shape=[stats, stats, stats],
        compiler_params=pltpu.CompilerParams(vmem_limit_bytes=48 * 1024 * 1024),
    )(queries, pairs, pairs)


def attend_far(queries, pairs, partial, head_dim, block_q=512):
    rows, width = queries.shape[1], queries.shape[2]
    heads = width // head_dim
    tile = pl.BlockSpec((block_q, head_dim), lambda h, i: (i, h))
    return pl.pallas_call(
        functools.partial(_attend_far_kernel, scaling=head_dim ** (-0.5)),
        grid=(heads, rows // block_q),
        in_specs=_attend_specs(queries, pairs, head_dim, block_q) + [tile, tile, tile],
        out_specs=tile,
        out_shape=jax.ShapeDtypeStruct((rows, width), jnp.bfloat16),
        compiler_params=pltpu.CompilerParams(vmem_limit_bytes=48 * 1024 * 1024),
    )(queries, pairs, pairs, *partial)


def tp_offsets(count, inner):
    return [(outer, step) for outer in range(count // inner) for step in range(inner)]


def tp_route(count, inner, offset):
    outer, step = offset
    groups = count // inner
    return [
        (i, ((i // inner + outer) % groups) * inner + (i % inner + step) % inner)
        for i in range(count)
    ]


def gather_by_distance(block, axis, inner):
    count = lax.axis_size(axis)
    offsets = tp_offsets(count, inner)
    received = [block]
    for offset in offsets[1:]:
        received.append(lax.ppermute(block, axis, tp_route(count, inner, offset)))
    return jnp.stack(received)


def scatter_by_distance(blocks, axis, inner):
    count = lax.axis_size(axis)
    offsets = tp_offsets(count, inner)
    groups = count // inner
    total = blocks[0].astype(jnp.float32)
    for outer, step in offsets[1:]:
        back = offsets.index(((groups - outer) % groups, (inner - step) % inner))
        arrived = lax.ppermute(blocks[back], axis, tp_route(count, inner, (outer, step)))
        total = total + arrived.astype(jnp.float32)
    return total


def body(inputs, modulation, w_qkv, w_attn_out, qk_gain, final_mod, w_final, w_embed, latent):
    head_dim = qk_gain.shape[2]
    x_rows = inputs[0]
    samples, tokens_local, width = x_rows.shape
    n_seq = lax.axis_size("seq")
    parts = n_seq // samples
    mod_rows = modulation[0]
    x_float = x_rows.astype(jnp.float32)
    x_mod = (
        layer_norm(x_float) * (1.0 + mod_rows[:, 1, None, :]) + mod_rows[:, 0, None, :]
    ).astype(jnp.bfloat16)
    weights = jnp.transpose(w_qkv[0], (1, 0, 2))
    local_width = weights.shape[2]
    norm_gains = qk_gain[0]
    gains = jnp.concatenate([norm_gains, jnp.ones_like(norm_gains[:1])], 0)
    ring = n_seq // parts
    ring_x = 4 if lax.axis_size("tp") % 4 == 0 else lax.axis_size("tp")
    groups = [list(range(p * ring, (p + 1) * ring)) for p in range(parts)]
    partner = [(i, (i + ring) % n_seq) for i in range(n_seq)]
    x_clip = lax.all_to_all(x_mod, "seq", 0, 0, tiled=True, axis_index_groups=groups)
    x_group = gather_by_distance(x_clip, "tp", ring_x)
    n_tp, n_src = x_group.shape[0], x_group.shape[1]
    rows = n_tp * n_src * tokens_local
    x_group = x_group.reshape(rows, width)
    pairs = project(x_group, weights, gains, head_dim, 1, 2)
    other = lax.ppermute(pairs, "seq", partner)
    queried = project(x_group, weights, gains, head_dim, 0, 1)
    partial = attend_own(queried, pairs, head_dim)
    attended = attend_far(queried, other, partial, head_dim)
    partial_out = jnp.einsum(
        "re,ed->rd", attended, w_attn_out[0], preferred_element_type=jnp.float32
    )
    branch_clip = scatter_by_distance(
        partial_out.astype(jnp.bfloat16).reshape(n_tp, n_src * tokens_local, width), "tp", ring_x
    ).astype(jnp.bfloat16).reshape(n_src, tokens_local, width)
    branch = (
        lax.all_to_all(branch_clip, "seq", 0, 0, tiled=True, axis_index_groups=groups)
        .reshape(samples, tokens_local, width)
        .astype(jnp.float32)
    )
    output = (x_float + mod_rows[:, 2, None, :] * branch).astype(jnp.bfloat16)
    final_in = (
        layer_norm(output.astype(jnp.float32)) * (1.0 + final_mod[:, 1, None, :])
        + final_mod[:, 0, None, :]
    ).astype(jnp.bfloat16)
    velocity = jnp.einsum("srd,dc->scr", final_in, w_final, preferred_element_type=jnp.float32)
    advanced = latent + step_size * velocity
    last_comp = lax.axis_size("comp") - 1
    position = lax.axis_index("comp")
    shared = jnp.stack([velocity, advanced]).astype(jnp.bfloat16)
    embedded = jnp.einsum(
        "scr,cd->srd", advanced.astype(jnp.bfloat16), w_embed, preferred_element_type=jnp.float32
    ).astype(jnp.bfloat16)
    sending = jnp.where(position == last_comp, embedded, output)
    packed = jnp.concatenate([sending.reshape(-1), shared.reshape(-1)])
    arrived = shifted(packed, "comp", 1)
    handed = arrived[: sending.size].reshape(sending.shape)
    from_last = arrived[sending.size :].reshape(shared.shape)
    shared = jnp.where(position == last_comp, shared, from_last).astype(jnp.float32)
    return (handed[None], shared[0], shared[1])


def solution(mesh):
    in_specs = (
        P("comp", None, ("seq", "tp"), None),
        P("comp", None, None, None),
        P("comp", None, None, "tp"),
        P("comp", "tp", None),
        P("comp", None, None),
        P(),
        P(),
        P(),
        P(None, None, ("seq", "tp")),
    )
    out_specs = (
        P("comp", None, ("seq", "tp"), None),
        P(None, None, ("seq", "tp")),
        P(None, None, ("seq", "tp")),
    )
    return jax.shard_map(body, mesh=mesh, in_specs=in_specs, out_specs=out_specs, check_vma=False)
```

```python
import jax
import jax.numpy as jnp
from jax import lax
import functools
from jax.experimental import pallas as pl
from jax.experimental.pallas import tpu as pltpu
from jax.sharding import PartitionSpec as P


step_size = 0.02
norm_eps = 1e-06


def shifted(block, axis, distance):
    devices = range(lax.axis_size(axis))
    route = [((i - distance) % len(devices), i) for i in devices]
    return lax.ppermute(block, axis, route)


def layer_norm(values):
    center = values - jnp.mean(values, -1, keepdims=True)
    return center * lax.rsqrt(jnp.mean(center * center, -1, keepdims=True) + norm_eps)


def _project_kernel(x_ref, w_ref, g_ref, o_ref, *, heads, head_dim, first):
    which = pl.program_id(0) + first
    mixed = jnp.dot(x_ref[...], w_ref[...], preferred_element_type=jnp.float32)
    gain = g_ref[pl.ds(which, 1), :]
    for h in range(heads):
        block = mixed[:, h * head_dim : (h + 1) * head_dim]
        normed = (
            block * lax.rsqrt(jnp.mean(block * block, -1, keepdims=True) + norm_eps) * gain
        )
        o_ref[:, h * head_dim : (h + 1) * head_dim] = jnp.where(
            which < 2, normed, block
        ).astype(o_ref.dtype)


def project(x, w, gains, head_dim, first, count):
    rows, width = x.shape
    local_width = w.shape[2]
    heads = local_width // head_dim
    kernel = functools.partial(_project_kernel, heads=heads, head_dim=head_dim, first=first)
    return pl.pallas_call(
        kernel,
        grid=(count,),
        in_specs=[
            pl.BlockSpec((rows, width), lambda c: (0, 0)),
            pl.BlockSpec((None, width, local_width), lambda c: (c + first, 0, 0)),
            pl.BlockSpec(gains.shape, lambda c: (0, 0)),
        ],
        out_specs=pl.BlockSpec((None, rows, local_width), lambda c: (c, 0, 0)),
        out_shape=jax.ShapeDtypeStruct((count, rows, local_width), jnp.bfloat16),
        compiler_params=pltpu.CompilerParams(vmem_limit_bytes=48 * 1024 * 1024),
    )(x, w, gains)


def _attend_own_kernel(q_ref, k_ref, v_ref, acc_ref, max_ref, sum_ref, *, scaling):
    scores = lax.dot_general(
        q_ref[...], k_ref[...], (((1,), (1,)), ((), ())), preferred_element_type=jnp.float32
    ) * scaling
    row_max = jnp.max(scores, -1, keepdims=True)
    weight = jnp.exp(scores - row_max)
    row_sum = jnp.sum(weight, -1, keepdims=True)
    acc_ref[...] = jnp.dot(
        weight.astype(jnp.bfloat16), v_ref[...], preferred_element_type=jnp.float32
    )
    max_ref[...] = jnp.broadcast_to(row_max, max_ref.shape)
    sum_ref[...] = jnp.broadcast_to(row_sum, sum_ref.shape)


def _attend_far_kernel(q_ref, k_ref, v_ref, acc_ref, max_ref, sum_ref, o_ref, *, scaling):
    scores = lax.dot_general(
        q_ref[...], k_ref[...], (((1,), (1,)), ((), ())), preferred_element_type=jnp.float32
    ) * scaling
    own_max = max_ref[:, :1]
    row_max = jnp.maximum(own_max, jnp.max(scores, -1, keepdims=True))
    rescale = jnp.exp(own_max - row_max)
    weight = jnp.exp(scores - row_max)
    row_sum = sum_ref[:, :1] * rescale + jnp.sum(weight, -1, keepdims=True)
    summed = acc_ref[...] * rescale + jnp.dot(
        weight.astype(jnp.bfloat16), v_ref[...], preferred_element_type=jnp.float32
    )
    o_ref[...] = (summed / row_sum).astype(o_ref.dtype)


def _attend_specs(pairs, head_dim, block_q):
    keys = pairs.shape[1]
    return [
        pl.BlockSpec((None, block_q, head_dim), lambda h, i: (0, i, h)),
        pl.BlockSpec((None, keys, head_dim), lambda h, i: (0, 0, h)),
        pl.BlockSpec((None, keys, head_dim), lambda h, i: (1, 0, h)),
    ]


def attend_own(queries, pairs, head_dim, block_q=512):
    rows, width = queries.shape[1], queries.shape[2]
    heads = width // head_dim
    tile = pl.BlockSpec((block_q, head_dim), lambda h, i: (i, h))
    stats = jax.ShapeDtypeStruct((rows, width), jnp.float32)
    return pl.pallas_call(
        functools.partial(_attend_own_kernel, scaling=head_dim ** (-0.5)),
        grid=(heads, rows // block_q),
        in_specs=_attend_specs(pairs, head_dim, block_q),
        out_specs=[tile, tile, tile],
        out_shape=[stats, stats, stats],
        compiler_params=pltpu.CompilerParams(vmem_limit_bytes=48 * 1024 * 1024),
    )(queries, pairs, pairs)


def attend_far(queries, pairs, partial, head_dim, block_q=512):
    rows, width = queries.shape[1], queries.shape[2]
    heads = width // head_dim
    tile = pl.BlockSpec((block_q, head_dim), lambda h, i: (i, h))
    return pl.pallas_call(
        functools.partial(_attend_far_kernel, scaling=head_dim ** (-0.5)),
        grid=(heads, rows // block_q),
        in_specs=_attend_specs(pairs, head_dim, block_q) + [tile, tile, tile],
        out_specs=tile,
        out_shape=jax.ShapeDtypeStruct((rows, width), jnp.bfloat16),
        compiler_params=pltpu.CompilerParams(vmem_limit_bytes=48 * 1024 * 1024),
    )(queries, pairs, pairs, *partial)


def issue_order(count):
    return [step for step in range(3, count)] + [step for step in range(1, 3)]


def gather_by_distance(block, axis):
    count = lax.axis_size(axis)
    received = {0: block}
    for step in issue_order(count):
        route = [(i, (i + step) % count) for i in range(count)]
        received[step] = lax.ppermute(block, axis, route)
    return jnp.stack([received[step] for step in range(count)])


def scatter_by_distance(blocks, axis):
    count = lax.axis_size(axis)
    arrived = {}
    for step in issue_order(count):
        route = [(i, (i + step) % count) for i in range(count)]
        arrived[step] = lax.ppermute(blocks[count - step], axis, route)
    total = blocks[0].astype(jnp.float32)
    for step in range(1, count):
        total = total + arrived[step].astype(jnp.float32)
    return total


def body(inputs, modulation, w_qkv, w_attn_out, qk_gain, final_mod, w_final, w_embed, latent):
    head_dim = qk_gain.shape[2]
    x_rows = inputs[0]
    samples, tokens_local, width = x_rows.shape
    n_seq = lax.axis_size("seq")
    parts = n_seq // samples
    mod_rows = modulation[0]
    x_float = x_rows.astype(jnp.float32)
    x_mod = (
        layer_norm(x_float) * (1.0 + mod_rows[:, 1, None, :]) + mod_rows[:, 0, None, :]
    ).astype(jnp.bfloat16)
    weights = jnp.transpose(w_qkv[0], (1, 0, 2))
    norm_gains = qk_gain[0]
    gains = jnp.concatenate([norm_gains, jnp.ones_like(norm_gains[:1])], 0)
    ring = n_seq // parts
    groups = [list(range(p * ring, (p + 1) * ring)) for p in range(parts)]
    partner = [(i, (i + ring) % n_seq) for i in range(n_seq)]
    x_clip = lax.all_to_all(x_mod, "seq", 0, 0, tiled=True, axis_index_groups=groups)
    x_group = gather_by_distance(x_clip, "tp")
    n_tp, n_src = x_group.shape[0], x_group.shape[1]
    rows = n_tp * n_src * tokens_local
    x_group = x_group.reshape(rows, width)
    pairs = project(x_group, weights, gains, head_dim, 1, 2)
    other = lax.ppermute(pairs, "seq", partner)
    queried = project(x_group, weights, gains, head_dim, 0, 1)
    partial = attend_own(queried, pairs, head_dim)
    attended = attend_far(queried, other, partial, head_dim)
    partial_out = jnp.einsum(
        "re,ed->rd", attended, w_attn_out[0], preferred_element_type=jnp.float32
    )
    branch_clip = scatter_by_distance(
        partial_out.astype(jnp.bfloat16).reshape(n_tp, n_src * tokens_local, width), "tp"
    ).astype(jnp.bfloat16).reshape(n_src, tokens_local, width)
    branch = (
        lax.all_to_all(branch_clip, "seq", 0, 0, tiled=True, axis_index_groups=groups)
        .reshape(samples, tokens_local, width)
        .astype(jnp.float32)
    )
    output = (x_float + mod_rows[:, 2, None, :] * branch).astype(jnp.bfloat16)
    final_in = (
        layer_norm(output.astype(jnp.float32)) * (1.0 + final_mod[:, 1, None, :])
        + final_mod[:, 0, None, :]
    ).astype(jnp.bfloat16)
    velocity = jnp.einsum("srd,dc->scr", final_in, w_final, preferred_element_type=jnp.float32)
    advanced = latent + step_size * velocity
    last_comp = lax.axis_size("comp") - 1
    position = lax.axis_index("comp")
    shared = jnp.stack([velocity, advanced]).astype(jnp.bfloat16)
    embedded = jnp.einsum(
        "scr,cd->srd", advanced.astype(jnp.bfloat16), w_embed, preferred_element_type=jnp.float32
    ).astype(jnp.bfloat16)
    sending = jnp.where(position == last_comp, embedded, output)
    packed = jnp.concatenate([sending.reshape(-1), shared.reshape(-1)])
    arrived = shifted(packed, "comp", 1)
    handed = arrived[: sending.size].reshape(sending.shape)
    from_last = arrived[sending.size :].reshape(shared.shape)
    shared = jnp.where(position == last_comp, shared, from_last).astype(jnp.float32)
    return (handed[None], shared[0], shared[1])


def solution(mesh):
    in_specs = (
        P("comp", None, ("seq", "tp"), None),
        P("comp", None, None, None),
        P("comp", None, None, "tp"),
        P("comp", "tp", None),
        P("comp", None, None),
        P(),
        P(),
        P(),
        P(None, None, ("seq", "tp")),
    )
    out_specs = (
        P("comp", None, ("seq", "tp"), None),
        P(None, None, ("seq", "tp")),
        P(None, None, ("seq", "tp")),
    )

    return jax.shard_map(body, mesh=mesh, in_specs=in_specs, out_specs=out_specs, check_vma=False)
```
